256 devices in a mesh: expert: 64 (over z, x, core), cuts: 4 (over y).
Axes of the slice: x: 4, y: 4, z: 8, core: 2. Of those that a mesh axis runs over, the one named last changes fastest.
Arguments:
- queries: bfloat16 [16384, 2048], P(('expert', 'cuts')), as said below
- new_keys: bfloat16 [16384, 2048], P(('expert', 'cuts')), as said below
- new_values: bfloat16 [16384, 2048], P(('expert', 'cuts')), may hold values from -6 to 6
- cache_keys: bfloat16 [131072, 2048], P(('expert', 'cuts')), as said below
- cache_values: bfloat16 [131072, 2048], P(('expert', 'cuts')), may hold values from -6 to 6
- parents: int32 [256, 64], P(('expert', 'cuts')), may hold values from 0 to 62, as said below
- tree_len: int32 [256], P(('expert', 'cuts')), may hold values from 32 to 64
- cache_len: int32 [256], P(('expert', 'cuts')), may hold values from 2 to 512
- accepted_path: int32 [256, 8], P(('expert', 'cuts')), may hold values from 0 to 31, as said below
- residual: bfloat16 [16384, 2048], P(('expert', 'cuts')), as said below
- norm_gain: float32 [2048], replicated, may hold values from 0.25 to 1.75
- out_weight: bfloat16 [2048, 2048], P('cuts'), may hold values from -0.125 to 0.125
- routes: int32 [16384, 4], P('expert'), may hold values from 0 to 63, as said below
- route_weights: float32 [16384, 4], P('expert'), may hold values from 0.05 to 0.6
- w_gate: bfloat16 [64, 2048, 1408], P('expert', None, 'cuts'), may hold values from -0.125 to 0.125
- w_up: bfloat16 [64, 2048, 1408], P('expert', None, 'cuts'), may hold values from -0.125 to 0.125
- w_down: bfloat16 [64, 1408, 2048], P('expert', 'cuts'), may hold values from -0.15625 to 0.15625
Outputs:
- layer_out: bfloat16 [16384, 2048], P(('expert', 'cuts'))
- accepted_kv: bfloat16 [2048, 4096], P(('expert', 'cuts'))
The draws below stay inside these ranges and needn't reach their ends.
Inputs may be any that keep to these rules, and one draw needn't show every extreme that they name: `parents`: the parent of slot 0 is 0; every other slot's parent is an earlier slot of the same request. `accepted_path`: each row starts at slot 0, each entry is the parent of the next one, and every entry is below the request's tree_len. `routes`: the 4 experts of a slot are distinct. Within each block of 64 consecutive rows (the tree slots of one device), no expert is named more than 8 times, and in every such block some expert is named exactly 8 times. `queries`: entries lie within -110 and 110. `new_keys`: entries lie within -6 and 6. `cache_keys`: entries lie within -4 and 4. `residual`: entries lie within -40 and 40.
All inputs are finite; a program needn't handle non-finite values.
Results may differ from the reference program's by a relative error of at most 0.014.
Values may be sent and summed in bfloat16 or wider, within the bound.
No kernel may reach another device: no remote copies, remote signals or barrier semaphores. Data moves between devices by JAX's collectives and lax.ppermute only.
A program may use at most 128 MiB of HBM per device.

```python
import math
import jax
import jax.numpy as jnp
from jax import lax

D = 2048
HEADS = 16
HEAD = 128
FF = 1408
TOPK = 4
TREE = 64
ACCEPT = 8
CACHE = 512
EXPERTS = 64
TOK_DEV = 64
REQ = 256
TOKENS = 16384
CAP = 8
N_CUTS = 4


def attention_bases(key):
    base_key = jax.random.fold_in(key, 11)
    first_key, second_key, third_key = jax.random.split(base_key, 3)
    query_base = jax.random.truncated_normal(first_key, -4.0, 4.0, (REQ, TREE, D), jnp.float32)
    cache_base = jax.random.truncated_normal(second_key, -4.0, 4.0, (REQ, CACHE, D), jnp.float32)
    noise = jax.random.truncated_normal(third_key, -4.0, 4.0, (REQ, TREE, D), jnp.float32)
    return (query_base, cache_base, noise)


def draw_queries(key, part):
    query_base, cache_base, noise = attention_bases(key)
    return query_base.reshape(TOKENS, D).astype(jnp.bfloat16)


def draw_new_keys(key, part):
    query_base, cache_base, noise = attention_bases(key)
    fresh = 0.35 * query_base + 0.9 * noise
    return fresh.reshape(TOKENS, D).astype(jnp.bfloat16)


def draw_cache_keys(key, part):
    query_base, cache_base, noise = attention_bases(key)
    return cache_base.reshape(REQ * CACHE, D).astype(jnp.bfloat16)


def draw_residual(key, part):
    base_key = jax.random.fold_in(key, 23)
    first_key = jax.random.fold_in(base_key, 0)
    values = jax.random.truncated_normal(first_key, -4.0, 4.0, (TOKENS, D), jnp.float32)
    return values.astype(jnp.bfloat16)


def tree_shape(key):
    base_key = jax.random.fold_in(key, 53)
    link_key, spine_key = jax.random.split(base_key)
    step_size = TREE // (2 * ACCEPT)
    slot_ids = jnp.arange(TREE, dtype=jnp.int32)
    link_bits = jax.random.randint(link_key, (REQ, TREE), 0, 1 << 30, dtype=jnp.int32)
    parents = link_bits % jnp.maximum(slot_ids, 1)[None, :]
    offsets = jax.random.randint(spine_key, (REQ, ACCEPT), 0, step_size, dtype=jnp.int32)
    offsets = offsets.at[0, ACCEPT - 1].set(step_size - 1)
    spine = jnp.arange(ACCEPT, dtype=jnp.int32)[None, :] * step_size + offsets
    spine = spine.at[:, 0].set(0)
    request_ids = jnp.arange(REQ, dtype=jnp.int32)[:, None]
    parents = parents.at[request_ids, spine[:, 1:]].set(spine[:, :-1])
    parents = parents.at[0, TREE - 1].set(TREE - 2)
    return (parents.astype(jnp.int32), spine.astype(jnp.int32))


def draw_parents(key, part):
    parents, spine = tree_shape(key)
    return parents


def draw_accepted_path(key, part):
    parents, spine = tree_shape(key)
    return spine


def block_order(order_key):
    return jax.random.permutation(order_key, TOK_DEV)


def draw_routes(key, part):
    base_key = jax.random.fold_in(key, 37)
    pair_key, count_key, heavy_key, order_key, turn_key = jax.random.split(base_key, 5)
    blocks = TOKENS // TOK_DEV
    half = CAP // 2
    pair_count = EXPERTS // 2
    hot_pairs = max(EXPERTS // 8, 1)
    pairing = jax.random.permutation(pair_key, EXPERTS)
    shifts = jax.random.randint(count_key, (blocks, pair_count), 0, half + 1, dtype=jnp.int32)
    heavy = jax.random.randint(heavy_key, (blocks, pair_count), CAP // 4, half + 1, dtype=jnp.int32)
    pair_ids = jnp.arange(pair_count, dtype=jnp.int32)[None, :]
    block_ids = jnp.arange(blocks, dtype=jnp.int32)[:, None]
    shifts = jnp.where(pair_ids < hot_pairs, heavy, shifts)
    shifts = jnp.where(block_ids == 0, 0, shifts)
    shifts = jnp.where(pair_ids == 0, half, shifts)
    counts = jnp.zeros((blocks, EXPERTS), jnp.int32)
    counts = counts.at[:, pairing[0::2]].set(half + shifts)
    counts = counts.at[:, pairing[1::2]].set(half - shifts)
    counts = counts.at[0, pairing[0]].set(0)
    counts = counts.at[0, pairing[1]].set(CAP)
    ends = jnp.cumsum(counts, axis=1)
    positions = jnp.arange(TOK_DEV * TOPK, dtype=jnp.int32)
    sequence = jnp.sum((ends[:, None, :] <= positions[None, :, None]).astype(jnp.int32), axis=2)
    table = sequence.reshape(blocks, TOPK, TOK_DEV).transpose(0, 2, 1)
    orders = jax.vmap(block_order)(jax.random.split(order_key, blocks))
    table = jnp.take_along_axis(table, orders[:, :, None], axis=1)
    turn = jax.random.randint(turn_key, (blocks, TOK_DEV, 1), 0, TOPK, dtype=jnp.int32)
    column = (jnp.arange(TOPK, dtype=jnp.int32)[None, None, :] + turn) % TOPK
    table = jnp.take_along_axis(table, column, axis=2)
    return table.reshape(TOKENS, TOPK).astype(jnp.int32)


def set_ends(values, key, low, top_value):
    longest = values.shape.index(max(values.shape))
    spots = []
    for shift in (0, 1):
        where = [jax.random.randint(jax.random.fold_in(key, axis), (), 0, length) for axis, length in enumerate(values.shape)]
        where[longest] = (where[longest] + shift) % values.shape[longest]
        spots.append(tuple(where))
    return values.at[spots[0]].set(low).at[spots[1]].set(top_value)


def block_scale(rng, extent, pieces, smallest, high):
    loudness, own = 1.0, jax.random.fold_in(rng, 6)
    for position, shards_of in pieces:
        heights = jnp.exp(jax.random.uniform(jax.random.fold_in(own, position), (shards_of,), jnp.float32, smallest / len(pieces), high / len(pieces)))
        loudness = loudness * jnp.repeat(heights, extent[position] // shards_of).reshape([-1 if axis == position else 1 for axis in range(len(extent))])
    return loudness


def centred(own_key, shape, scale, bound, shards=(), held_as=jnp.bfloat16):
    entries = scale * jax.random.normal(own_key, shape, jnp.float32)
    if shards:
        entries = entries * block_scale(own_key, shape, shards, -0.22, 0.18)
    return jnp.clip(entries, -bound, bound).astype(held_as)


def setup_inputs(seed: int = 0) -> dict:
    splits = jax.random.split(jax.random.key(seed), 18)
    queries = draw_queries(jax.random.fold_in(splits[17], 71), 0)
    new_keys = draw_new_keys(jax.random.fold_in(splits[17], 71), 0)
    new_values = centred(splits[2], (TOKENS, D), 1.0, 6.0, ((0, 256),))
    cache_keys = draw_cache_keys(jax.random.fold_in(splits[17], 71), 0)
    cache_values = centred(splits[4], (REQ * CACHE, D), 1.0, 6.0, ((0, 256),))
    parents = draw_parents(jax.random.fold_in(splits[17], 71), 0)
    tree_len = set_ends(jax.random.randint(splits[6], (REQ,), TREE // 2, TREE + 1), jax.random.fold_in(splits[6], 1), TREE // 2, TREE).astype(jnp.int32)
    cache_len = set_ends(jax.random.randint(splits[7], (REQ,), 2, CACHE + 1), jax.random.fold_in(splits[7], 1), 2, CACHE).astype(jnp.int32)
    accepted_path = draw_accepted_path(jax.random.fold_in(splits[17], 71), 0)
    residual = draw_residual(jax.random.fold_in(splits[17], 71), 0)
    norm_gain = jnp.clip(1.0 + 0.15 * jax.random.normal(splits[10], (D,), jnp.float32), 0.25, 1.75)
    out_weight = centred(splits[11], (D, D), D ** -0.5, 0.125, ((0, 4),))
    routes = draw_routes(jax.random.fold_in(splits[17], 71), 0)
    route_weights = jnp.clip(jnp.exp(math.log(0.6) - 2.4849067 * jax.random.uniform(splits[13], (TOKENS, TOPK), jnp.float32) ** block_scale(splits[13], (TOKENS, TOPK), ((0, 64),), -0.2, 0.2)), 0.05, 0.6)
    w_gate = centred(splits[14], (EXPERTS, D, FF), D ** -0.5, 0.125, ((0, 64), (2, 4)))
    w_up = centred(splits[15], (EXPERTS, D, FF), D ** -0.5, 0.125, ((0, 64), (2, 4)))
    w_down = centred(splits[16], (EXPERTS, FF, D), FF ** -0.5, 0.15625, ((0, 64), (1, 4)))
    return {"queries": queries, "new_keys": new_keys, "new_values": new_values, "cache_keys": cache_keys, "cache_values": cache_values, "parents": parents, "tree_len": tree_len, "cache_len": cache_len, "accepted_path": accepted_path, "residual": residual, "norm_gain": norm_gain, "out_weight": out_weight, "routes": routes, "route_weights": route_weights, "w_gate": w_gate, "w_up": w_up, "w_down": w_down}


epsilon = 1e-06

def ancestors(parents):
    slot_ids = jnp.arange(TREE, dtype=jnp.int32)
    linked = (parents[:, None] == slot_ids[None, :]) | (slot_ids[:, None] == slot_ids[None, :])
    reach = linked.astype(jnp.float32)
    for doubling in range(TREE.bit_length()):
        reach = jnp.minimum(jnp.dot(reach, reach, precision=lax.Precision.HIGHEST), 1.0)
    return reach > 0.5

def tree_attention(request):
    queries, new_keys, new_values, cache_keys, cache_values, parents, tree_len, cache_len = request
    query_heads = queries.reshape(TREE, HEADS, HEAD).astype(jnp.float32)
    cache_heads = cache_keys.reshape(CACHE, HEADS, HEAD).astype(jnp.float32)
    fresh_heads = new_keys.reshape(TREE, HEADS, HEAD).astype(jnp.float32)
    score_scale = 1.0 / math.sqrt(HEAD)
    cache_scores = jnp.einsum('qhd,khd->hqk', query_heads, cache_heads) * score_scale
    fresh_scores = jnp.einsum('qhd,khd->hqk', query_heads, fresh_heads) * score_scale
    slot_ids = jnp.arange(TREE, dtype=jnp.int32)
    cache_seen = jnp.arange(CACHE, dtype=jnp.int32) < cache_len
    fresh_seen = ancestors(parents) & (slot_ids[None, :] < tree_len)
    cache_scores = jnp.where(cache_seen[None, None, :], cache_scores, -jnp.inf)
    fresh_scores = jnp.where(fresh_seen[None, :, :], fresh_scores, -jnp.inf)
    highest = jnp.maximum(lax.optimization_barrier(jnp.max(cache_scores, axis=2)), lax.optimization_barrier(jnp.max(fresh_scores, axis=2)))[:, :, None]
    cache_exp = jnp.exp(cache_scores - highest)
    fresh_exp = jnp.exp(fresh_scores - highest)
    total = lax.optimization_barrier(jnp.sum(cache_exp, axis=2, keepdims=True)) + lax.optimization_barrier(jnp.sum(fresh_exp, axis=2, keepdims=True))
    cache_weights = (cache_exp / total).astype(jnp.bfloat16).astype(jnp.float32)
    fresh_weights = (fresh_exp / total).astype(jnp.bfloat16).astype(jnp.float32)
    cache_vals = cache_values.reshape(CACHE, HEADS, HEAD).astype(jnp.float32)
    fresh_vals = new_values.reshape(TREE, HEADS, HEAD).astype(jnp.float32)
    mixed = jnp.einsum('hqk,khd->qhd', cache_weights, cache_vals)
    mixed = mixed + jnp.einsum('hqk,khd->qhd', fresh_weights, fresh_vals)
    return mixed.reshape(TREE, D).astype(jnp.bfloat16)

def reference(queries, new_keys, new_values, cache_keys, cache_values, parents, tree_len, cache_len, accepted_path, residual, norm_gain, out_weight, routes, route_weights, w_gate, w_up, w_down):
    attended = lax.map(tree_attention, (queries.reshape(REQ, TREE, D), new_keys.reshape(REQ, TREE, D), new_values.reshape(REQ, TREE, D), cache_keys.reshape(REQ, CACHE, D), cache_values.reshape(REQ, CACHE, D), parents, tree_len, cache_len))
    attended = attended.reshape(TOKENS, D)
    stream = residual.astype(jnp.float32) + jnp.dot(attended, out_weight, preferred_element_type=jnp.float32)
    power = lax.optimization_barrier(jnp.mean(stream * stream, axis=1, keepdims=True))
    normed = (stream * lax.rsqrt(power + epsilon) * norm_gain).astype(jnp.bfloat16)
    blocks = TOKENS // TOK_DEV
    flat = routes.reshape(blocks, TOK_DEV * TOPK)
    onehot = (flat[:, :, None] == jnp.arange(EXPERTS, dtype=jnp.int32)[None, None, :]).astype(jnp.int32)
    ahead = jnp.cumsum(onehot, axis=1) - onehot
    slot_of = lax.optimization_barrier(jnp.sum(ahead * onehot, axis=2))
    column = jnp.arange(blocks, dtype=jnp.int32)[:, None] * CAP + slot_of
    token_of = (jnp.arange(TOKENS * TOPK, dtype=jnp.int32) // TOPK).reshape(blocks, TOK_DEV * TOPK)
    table = jnp.full((EXPERTS, blocks * CAP), -1, jnp.int32).at[flat, column].set(token_of)
    gains = jnp.zeros((EXPERTS, blocks * CAP), jnp.float32).at[flat, column].set(route_weights.reshape(blocks, TOK_DEV * TOPK))
    slice_width = FF // N_CUTS

    def one_expert(total, item):
        rows_of, gain_row, gate_w, up_w, down_w = item
        used = rows_of >= 0
        safe_rows = jnp.maximum(rows_of, 0)
        picked = jnp.where(used[:, None], normed[safe_rows], jnp.zeros((), jnp.bfloat16))
        gate = jnp.dot(picked, gate_w, preferred_element_type=jnp.float32)
        upper = jnp.dot(picked, up_w, preferred_element_type=jnp.float32)
        hidden = (jax.nn.silu(gate) * upper).astype(jnp.bfloat16)
        expert_out = jnp.zeros((picked.shape[0], D), jnp.float32)
        for piece_idx in range(N_CUTS):
            lower = piece_idx * slice_width
            piece = jnp.dot(hidden[:, lower:lower + slice_width], down_w[lower:lower + slice_width], preferred_element_type=jnp.float32).astype(jnp.bfloat16)
            piece = lax.optimization_barrier(piece)
            expert_out = expert_out + piece.astype(jnp.float32)
        total = total.at[safe_rows].add(gain_row[:, None] * expert_out)
        return (total, None)
    moe, unused = lax.scan(one_expert, jnp.zeros((TOKENS, D), jnp.float32), (table, gains, w_gate, w_up, w_down))
    layer_out = (stream + moe).astype(jnp.bfloat16)
    picks = (jnp.arange(REQ, dtype=jnp.int32)[:, None] * TREE + accepted_path).reshape(-1)
    accepted_kv = jnp.concatenate([new_keys[picks], new_values[picks]], axis=1)
    return (layer_out, accepted_kv)
```

```python
import math

import jax
import jax.numpy as jnp
from jax import lax
from jax.sharding import PartitionSpec as P

HEADS = 16
HEAD = 128
TOPK = 4
TREE = 64
CAP = 8


epsilon = 1e-06


def ancestors(parents):
    slot_ids = jnp.arange(TREE, dtype=jnp.int32)
    linked = (parents[:, None] == slot_ids[None, :]) | (slot_ids[:, None] == slot_ids[None, :])
    reach = linked.astype(jnp.float32)
    for doubling in range(TREE.bit_length()):
        reach = jnp.minimum(jnp.dot(reach, reach, precision=lax.Precision.HIGHEST), 1.0)
    return reach > 0.5


def tree_attention(request):
    queries, new_keys, new_values, cache_keys, cache_values, parents, tree_len, cache_len = request
    cache_rows = cache_keys.shape[0]
    query_heads = queries.reshape(TREE, HEADS, HEAD)
    cache_heads = cache_keys.reshape(cache_rows, HEADS, HEAD)
    fresh_heads = new_keys.reshape(TREE, HEADS, HEAD)
    score_scale = 1.0 / math.sqrt(HEAD)
    cache_scores = (
        jnp.einsum("qhd,khd->hqk", query_heads, cache_heads, preferred_element_type=jnp.float32)
        * score_scale
    )
    fresh_scores = (
        jnp.einsum("qhd,khd->hqk", query_heads, fresh_heads, preferred_element_type=jnp.float32)
        * score_scale
    )
    slot_ids = jnp.arange(TREE, dtype=jnp.int32)
    cache_seen = jnp.arange(cache_rows, dtype=jnp.int32) < cache_len
    fresh_seen = ancestors(parents) & (slot_ids[None, :] < tree_len)
    cache_scores = jnp.where(cache_seen[None, None, :], cache_scores, -jnp.inf)
    fresh_scores = jnp.where(fresh_seen[None, :, :], fresh_scores, -jnp.inf)
    highest = jnp.maximum(jnp.max(cache_scores, axis=2), jnp.max(fresh_scores, axis=2))[:, :, None]
    cache_exp = jnp.exp(cache_scores - highest)
    fresh_exp = jnp.exp(fresh_scores - highest)
    total = jnp.sum(cache_exp, axis=2, keepdims=True) + jnp.sum(fresh_exp, axis=2, keepdims=True)
    cache_weights = (cache_exp / total).astype(jnp.bfloat16)
    fresh_weights = (fresh_exp / total).astype(jnp.bfloat16)
    mixed = jnp.einsum(
        "hqk,khd->qhd",
        cache_weights,
        cache_values.reshape(cache_rows, HEADS, HEAD),
        preferred_element_type=jnp.float32,
    )
    mixed = mixed + jnp.einsum(
        "hqk,khd->qhd",
        fresh_weights,
        new_values.reshape(TREE, HEADS, HEAD),
        preferred_element_type=jnp.float32,
    )
    return mixed.reshape(TREE, HEADS * HEAD).astype(jnp.bfloat16)


def expert_rows(flat_in, gate_w, up_w, down_w):
    gate = jnp.dot(flat_in, gate_w, preferred_element_type=jnp.float32)
    upper = jnp.dot(flat_in, up_w, preferred_element_type=jnp.float32)
    hidden = (jax.nn.silu(gate) * upper).astype(jnp.bfloat16)
    return jnp.dot(hidden, down_w, preferred_element_type=jnp.float32)


def norm_rows(stream, norm_gain):
    power = jnp.mean(stream * stream, axis=1, keepdims=True)
    return (stream * lax.rsqrt(power + epsilon) * norm_gain).astype(jnp.bfloat16)


def on_device(
    queries,
    new_keys,
    new_values,
    cache_keys,
    cache_values,
    parents,
    tree_len,
    cache_len,
    accepted_path,
    residual,
    norm_gain,
    out_weight,
    routes,
    route_weights,
    w_gate,
    w_up,
    w_down,
):
    place = lax.axis_index("cuts")
    tok_rows = queries.shape[0]
    requests = tok_rows // TREE
    cache_rows = cache_keys.shape[0] // requests
    width = queries.shape[1]
    attended = lax.map(
        tree_attention,
        (
            queries.reshape(requests, TREE, width),
            new_keys.reshape(requests, TREE, width),
            new_values.reshape(requests, TREE, width),
            cache_keys.reshape(requests, cache_rows, width),
            cache_values.reshape(requests, cache_rows, width),
            parents,
            tree_len,
            cache_len,
        ),
    )
    attended = attended.reshape(tok_rows, width)
    head_group = lax.all_to_all(attended, "cuts", split_axis=1, concat_axis=0, tiled=True)
    projected = jnp.dot(head_group, out_weight, preferred_element_type=jnp.float32)
    projected_own = lax.psum_scatter(
        projected.astype(jnp.bfloat16), "cuts", scatter_dimension=0, tiled=True
    )
    stream = residual.astype(jnp.float32) + projected_own.astype(jnp.float32)
    normed = norm_rows(stream, norm_gain)

    experts_all = w_gate.shape[0] * lax.axis_size("expert")
    capacity = CAP
    start = place * tok_rows
    own_routes = lax.dynamic_slice_in_dim(routes, start, tok_rows, 0)
    own_gains = lax.dynamic_slice_in_dim(route_weights, start, tok_rows, 0)
    flat = own_routes.reshape(tok_rows * TOPK)
    onehot = (flat[:, None] == jnp.arange(experts_all, dtype=jnp.int32)[None, :]).astype(jnp.int32)
    ahead = jnp.cumsum(onehot, axis=0) - onehot
    slot_of = jnp.sum(ahead * onehot, axis=1)
    dest = flat * capacity + slot_of
    token_of = jnp.arange(tok_rows * TOPK, dtype=jnp.int32) // TOPK
    table = jnp.full((experts_all * capacity,), -1, jnp.int32).at[dest].set(token_of)
    filled = table >= 0
    outgoing = jnp.where(
        filled[:, None], normed[jnp.maximum(table, 0)], jnp.zeros((), jnp.bfloat16)
    )
    outgoing = outgoing.reshape(experts_all, capacity, width)
    arrived = lax.all_to_all(outgoing, "expert", split_axis=0, concat_axis=0, tiled=True)
    gathered = lax.all_gather(arrived, "cuts", axis=0, tiled=True)
    product = expert_rows(gathered.reshape(-1, width), w_gate[0], w_up[0], w_down[0])
    pieces = product.astype(jnp.bfloat16)
    summed = lax.psum_scatter(pieces, "cuts", scatter_dimension=0, tiled=True)
    returned = lax.all_to_all(
        summed.reshape(experts_all, capacity, width), "expert", split_axis=0, concat_axis=0, tiled=True
    )
    picked = returned.reshape(-1, width)[dest].reshape(tok_rows, TOPK, width)
    moe = jnp.sum(own_gains[:, :, None] * picked.astype(jnp.float32), axis=1)
    layer_out = (stream + moe).astype(jnp.bfloat16)
    picks = (jnp.arange(requests, dtype=jnp.int32)[:, None] * TREE + accepted_path).reshape(-1)
    accepted_kv = jnp.concatenate([new_keys[picks], new_values[picks]], axis=1)
    return (layer_out, accepted_kv)


def solution(mesh):
    placed = (
        P(("expert", "cuts"), None),
        P(("expert", "cuts"), None),
        P(("expert", "cuts"), None),
        P(("expert", "cuts"), None),
        P(("expert", "cuts"), None),
        P(("expert", "cuts"), None),
        P(("expert", "cuts")),
        P(("expert", "cuts")),
        P(("expert", "cuts"), None),
        P(("expert", "cuts"), None),
        P(),
        P("cuts", None),
        P("expert", None),
        P("expert", None),
        P("expert", None, "cuts"),
        P("expert", None, "cuts"),
        P("expert", "cuts", None),
    )
    return jax.shard_map(
        on_device,
        mesh=mesh,
        in_specs=placed,
        out_specs=(P(("expert", "cuts"), None), P(("expert", "cuts"), None)),
        check_vma=False,
    )
```

```python
import math

import jax
import jax.numpy as jnp
from jax import lax
from jax.sharding import PartitionSpec as P

HEADS = 16
HEAD = 128
TOPK = 4
TREE = 64
CAP = 8
N_CHUNKS = 2


epsilon = 1e-06


def ancestors(parents):
    slot_ids = jnp.arange(TREE, dtype=jnp.int32)
    linked = (parents[:, None] == slot_ids[None, :]) | (slot_ids[:, None] == slot_ids[None, :])
    reach = linked.astype(jnp.float32)
    for doubling in range(TREE.bit_length()):
        reach = jnp.minimum(jnp.dot(reach, reach, precision=lax.Precision.HIGHEST), 1.0)
    return reach > 0.5


def tree_attention(request):
    queries, new_keys, new_values, cache_keys, cache_values, parents, tree_len, cache_len = request
    cache_rows = cache_keys.shape[0]
    query_heads = queries.reshape(TREE, HEADS, HEAD)
    cache_heads = cache_keys.reshape(cache_rows, HEADS, HEAD)
    fresh_heads = new_keys.reshape(TREE, HEADS, HEAD)
    score_scale = 1.0 / math.sqrt(HEAD)
    cache_scores = (
        jnp.einsum("qhd,khd->hqk", query_heads, cache_heads, preferred_element_type=jnp.float32)
        * score_scale
    )
    fresh_scores = (
        jnp.einsum("qhd,khd->hqk", query_heads, fresh_heads, preferred_element_type=jnp.float32)
        * score_scale
    )
    slot_ids = jnp.arange(TREE, dtype=jnp.int32)
    cache_seen = jnp.arange(cache_rows, dtype=jnp.int32) < cache_len
    fresh_seen = ancestors(parents) & (slot_ids[None, :] < tree_len)
    cache_scores = jnp.where(cache_seen[None, None, :], cache_scores, -jnp.inf)
    fresh_scores = jnp.where(fresh_seen[None, :, :], fresh_scores, -jnp.inf)
    highest = jnp.maximum(jnp.max(cache_scores, axis=2), jnp.max(fresh_scores, axis=2))[:, :, None]
    cache_exp = jnp.exp(cache_scores - highest)
    fresh_exp = jnp.exp(fresh_scores - highest)
    total = jnp.sum(cache_exp, axis=2, keepdims=True) + jnp.sum(fresh_exp, axis=2, keepdims=True)
    cache_weights = (cache_exp / total).astype(jnp.bfloat16)
    fresh_weights = (fresh_exp / total).astype(jnp.bfloat16)
    mixed = jnp.einsum(
        "hqk,khd->qhd",
        cache_weights,
        cache_values.reshape(cache_rows, HEADS, HEAD),
        preferred_element_type=jnp.float32,
    )
    mixed = mixed + jnp.einsum(
        "hqk,khd->qhd",
        fresh_weights,
        new_values.reshape(TREE, HEADS, HEAD),
        preferred_element_type=jnp.float32,
    )
    return mixed.reshape(TREE, HEADS * HEAD).astype(jnp.bfloat16)


def expert_rows(flat_in, gate_w, up_w, down_w):
    gate = jnp.dot(flat_in, gate_w, preferred_element_type=jnp.float32)
    upper = jnp.dot(flat_in, up_w, preferred_element_type=jnp.float32)
    hidden = (jax.nn.silu(gate) * upper).astype(jnp.bfloat16)
    return jnp.dot(hidden, down_w, preferred_element_type=jnp.float32)


def norm_rows(stream, norm_gain):
    power = jnp.mean(stream * stream, axis=1, keepdims=True)
    return (stream * lax.rsqrt(power + epsilon) * norm_gain).astype(jnp.bfloat16)


def on_device(
    queries,
    new_keys,
    new_values,
    cache_keys,
    cache_values,
    parents,
    tree_len,
    cache_len,
    accepted_path,
    residual,
    norm_gain,
    out_weight,
    routes,
    route_weights,
    w_gate,
    w_up,
    w_down,
):
    place = lax.axis_index("cuts")
    tok_rows = queries.shape[0]
    requests = tok_rows // TREE
    cache_rows = cache_keys.shape[0] // requests
    width = queries.shape[1]
    attended = lax.map(
        tree_attention,
        (
            queries.reshape(requests, TREE, width),
            new_keys.reshape(requests, TREE, width),
            new_values.reshape(requests, TREE, width),
            cache_keys.reshape(requests, cache_rows, width),
            cache_values.reshape(requests, cache_rows, width),
            parents,
            tree_len,
            cache_len,
        ),
    )
    attended = attended.reshape(tok_rows, width)
    head_group = lax.all_to_all(attended, "cuts", split_axis=1, concat_axis=0, tiled=True)
    projected = jnp.dot(head_group, out_weight, preferred_element_type=jnp.float32)
    projected_own = lax.psum_scatter(
        projected.astype(jnp.bfloat16), "cuts", scatter_dimension=0, tiled=True
    )
    stream = residual.astype(jnp.float32) + projected_own.astype(jnp.float32)
    normed = norm_rows(stream, norm_gain)

    experts_all = w_gate.shape[0] * lax.axis_size("expert")
    capacity = CAP
    start = place * tok_rows
    own_routes = lax.dynamic_slice_in_dim(routes, start, tok_rows, 0)
    own_gains = lax.dynamic_slice_in_dim(route_weights, start, tok_rows, 0)
    flat = own_routes.reshape(tok_rows * TOPK)
    onehot = (flat[:, None] == jnp.arange(experts_all, dtype=jnp.int32)[None, :]).astype(jnp.int32)
    ahead = jnp.cumsum(onehot, axis=0) - onehot
    slot_of = jnp.sum(ahead * onehot, axis=1)
    dest = flat * capacity + slot_of
    token_of = jnp.arange(tok_rows * TOPK, dtype=jnp.int32) // TOPK
    table = jnp.full((experts_all * capacity,), -1, jnp.int32).at[dest].set(token_of)
    filled = table >= 0
    outgoing = jnp.where(
        filled[:, None], normed[jnp.maximum(table, 0)], jnp.zeros((), jnp.bfloat16)
    )
    outgoing = outgoing.reshape(experts_all, capacity, width)
    chunk = capacity // N_CHUNKS
    returned_parts = []
    for part in range(N_CHUNKS):
        sending = outgoing[:, part * chunk:(part + 1) * chunk]
        arrived = lax.all_to_all(sending, "expert", split_axis=0, concat_axis=0, tiled=True)
        gathered = lax.all_gather(arrived, "cuts", axis=0, tiled=True)
        product = expert_rows(gathered.reshape(-1, width), w_gate[0], w_up[0], w_down[0])
        pieces = product.astype(jnp.bfloat16)
        summed = lax.psum_scatter(pieces, "cuts", scatter_dimension=0, tiled=True)
        returned_parts.append(
            lax.all_to_all(
                summed.reshape(experts_all, chunk, width), "expert", split_axis=0, concat_axis=0, tiled=True
            )
        )
    returned = jnp.concatenate(returned_parts, axis=1)
    picked = returned.reshape(-1, width)[dest].reshape(tok_rows, TOPK, width)
    moe = jnp.sum(own_gains[:, :, None] * picked.astype(jnp.float32), axis=1)
    layer_out = (stream + moe).astype(jnp.bfloat16)
    picks = (jnp.arange(requests, dtype=jnp.int32)[:, None] * TREE + accepted_path).reshape(-1)
    accepted_kv = jnp.concatenate([new_keys[picks], new_values[picks]], axis=1)
    return (layer_out, accepted_kv)


def solution(mesh):
    placed = (
        P(("expert", "cuts"), None),
        P(("expert", "cuts"), None),
        P(("expert", "cuts"), None),
        P(("expert", "cuts"), None),
        P(("expert", "cuts"), None),
        P(("expert", "cuts"), None),
        P(("expert", "cuts")),
        P(("expert", "cuts")),
        P(("expert", "cuts"), None),
        P(("expert", "cuts"), None),
        P(),
        P("cuts", None),
        P("expert", None),
        P("expert", None),
        P("expert", None, "cuts"),
        P("expert", None, "cuts"),
        P("expert", "cuts", None),
    )
    return jax.shard_map(
        on_device,
        mesh=mesh,
        in_specs=placed,
        out_specs=(P(("expert", "cuts"), None), P(("expert", "cuts"), None)),
        check_vma=False,
    )
```

```python
import math

import jax
import jax.numpy as jnp
from jax import lax
from jax.sharding import PartitionSpec as P

HEADS = 16
HEAD = 128
TOPK = 4
TREE = 64
CAP = 8
N_CHUNKS = 2


epsilon = 1e-06


def ancestors(parents):
    slot_ids = jnp.arange(TREE, dtype=jnp.int32)
    linked = (parents[:, None] == slot_ids[None, :]) | (slot_ids[:, None] == slot_ids[None, :])
    reach = linked.astype(jnp.float32)
    for doubling in range(TREE.bit_length()):
        reach = jnp.minimum(jnp.dot(reach, reach, precision=lax.Precision.HIGHEST), 1.0)
    return reach > 0.5


def tree_attention(request):
    queries, new_keys, new_values, cache_keys, cache_values, parents, tree_len, cache_len = request
    cache_rows = cache_keys.shape[0]
    query_heads = queries.reshape(TREE, HEADS, HEAD)
    cache_heads = cache_keys.reshape(cache_rows, HEADS, HEAD)
    fresh_heads = new_keys.reshape(TREE, HEADS, HEAD)
    score_scale = 1.0 / math.sqrt(HEAD)
    cache_scores = (
        jnp.einsum("qhd,khd->hqk", query_heads, cache_heads, preferred_element_type=jnp.float32)
        * score_scale
    )
    fresh_scores = (
        jnp.einsum("qhd,khd->hqk", query_heads, fresh_heads, preferred_element_type=jnp.float32)
        * score_scale
    )
    slot_ids = jnp.arange(TREE, dtype=jnp.int32)
    cache_seen = jnp.arange(cache_rows, dtype=jnp.int32) < cache_len
    fresh_seen = ancestors(parents) & (slot_ids[None, :] < tree_len)
    cache_scores = jnp.where(cache_seen[None, None, :], cache_scores, -jnp.inf)
    fresh_scores = jnp.where(fresh_seen[None, :, :], fresh_scores, -jnp.inf)
    highest = jnp.maximum(jnp.max(cache_scores, axis=2), jnp.max(fresh_scores, axis=2))[:, :, None]
    cache_exp = jnp.exp(cache_scores - highest)
    fresh_exp = jnp.exp(fresh_scores - highest)
    total = jnp.sum(cache_exp, axis=2, keepdims=True) + jnp.sum(fresh_exp, axis=2, keepdims=True)
    cache_weights = (cache_exp / total).astype(jnp.bfloat16)
    fresh_weights = (fresh_exp / total).astype(jnp.bfloat16)
    mixed = jnp.einsum(
        "hqk,khd->qhd",
        cache_weights,
        cache_values.reshape(cache_rows, HEADS, HEAD),
        preferred_element_type=jnp.float32,
    )
    mixed = mixed + jnp.einsum(
        "hqk,khd->qhd",
        fresh_weights,
        new_values.reshape(TREE, HEADS, HEAD),
        preferred_element_type=jnp.float32,
    )
    return mixed.reshape(TREE, HEADS * HEAD).astype(jnp.bfloat16)


def expert_rows(flat_in, gate_w, up_w, down_w):
    gate = jnp.dot(flat_in, gate_w, preferred_element_type=jnp.float32)
    upper = jnp.dot(flat_in, up_w, preferred_element_type=jnp.float32)
    hidden = (jax.nn.silu(gate) * upper).astype(jnp.bfloat16)
    return jnp.dot(hidden, down_w, preferred_element_type=jnp.float32)


def norm_rows(stream, norm_gain):
    power = jnp.mean(stream * stream, axis=1, keepdims=True)
    return (stream * lax.rsqrt(power + epsilon) * norm_gain).astype(jnp.bfloat16)


def on_device(
    queries,
    new_keys,
    new_values,
    cache_keys,
    cache_values,
    parents,
    tree_len,
    cache_len,
    accepted_path,
    residual,
    norm_gain,
    out_weight,
    routes,
    route_weights,
    w_gate,
    w_up,
    w_down,
):
    place = lax.axis_index("cuts")
    tok_rows = queries.shape[0]
    requests = tok_rows // TREE
    cache_rows = cache_keys.shape[0] // requests
    width = queries.shape[1]
    attended = lax.map(
        tree_attention,
        (
            queries.reshape(requests, TREE, width),
            new_keys.reshape(requests, TREE, width),
            new_values.reshape(requests, TREE, width),
            cache_keys.reshape(requests, cache_rows, width),
            cache_values.reshape(requests, cache_rows, width),
            parents,
            tree_len,
            cache_len,
        ),
    )
    attended = attended.reshape(tok_rows, width)
    head_group = lax.all_to_all(attended, "cuts", split_axis=1, concat_axis=0, tiled=True)
    gate_full = lax.all_gather(w_gate[0], "cuts", axis=0)
    up_full = lax.all_gather(w_up[0], "cuts", axis=0)
    down_full = lax.all_gather(w_down[0], "cuts", axis=0)
    projected = jnp.dot(head_group, out_weight, preferred_element_type=jnp.float32)
    partials = lax.all_to_all(
        projected.astype(jnp.bfloat16).reshape(lax.axis_size("cuts"), tok_rows, width),
        "cuts",
        split_axis=0,
        concat_axis=0,
        tiled=True,
    )
    stream = residual.astype(jnp.float32) + jnp.sum(partials.astype(jnp.float32), axis=0)
    normed = norm_rows(stream, norm_gain)

    experts_all = w_gate.shape[0] * lax.axis_size("expert")
    capacity = CAP
    start = place * tok_rows
    own_routes = lax.dynamic_slice_in_dim(routes, start, tok_rows, 0)
    own_gains = lax.dynamic_slice_in_dim(route_weights, start, tok_rows, 0)
    flat = own_routes.reshape(tok_rows * TOPK)
    onehot = (flat[:, None] == jnp.arange(experts_all, dtype=jnp.int32)[None, :]).astype(jnp.int32)
    ahead = jnp.cumsum(onehot, axis=0) - onehot
    slot_of = jnp.sum(ahead * onehot, axis=1)
    dest = flat * capacity + slot_of
    token_of = jnp.arange(tok_rows * TOPK, dtype=jnp.int32) // TOPK
    table = jnp.full((experts_all * capacity,), -1, jnp.int32).at[dest].set(token_of)
    filled = table >= 0
    outgoing = jnp.where(
        filled[:, None], normed[jnp.maximum(table, 0)], jnp.zeros((), jnp.bfloat16)
    )
    outgoing = outgoing.reshape(experts_all, capacity, width)
    arrived = lax.all_to_all(outgoing, "expert", split_axis=0, concat_axis=0, tiled=True)
    rows = arrived.reshape(-1, width)
    gate = jnp.einsum("rd,cdf->rcf", rows, gate_full, preferred_element_type=jnp.float32)
    upper = jnp.einsum("rd,cdf->rcf", rows, up_full, preferred_element_type=jnp.float32)
    hidden = (jax.nn.silu(gate) * upper).astype(jnp.bfloat16)
    product = jnp.einsum("rcf,cfd->rd", hidden, down_full, preferred_element_type=jnp.float32)
    returned = lax.all_to_all(
        product.astype(jnp.bfloat16).reshape(experts_all, capacity, width),
        "expert",
        split_axis=0,
        concat_axis=0,
        tiled=True,
    )
    picked = returned.reshape(-1, width)[dest].reshape(tok_rows, TOPK, width)
    moe = jnp.sum(own_gains[:, :, None] * picked.astype(jnp.float32), axis=1)
    layer_out = (stream + moe).astype(jnp.bfloat16)
    picks = (jnp.arange(requests, dtype=jnp.int32)[:, None] * TREE + accepted_path).reshape(-1)
    accepted_kv = jnp.concatenate([new_keys[picks], new_values[picks]], axis=1)
    return (layer_out, accepted_kv)


def solution(mesh):
    placed = (
        P(("expert", "cuts"), None),
        P(("expert", "cuts"), None),
        P(("expert", "cuts"), None),
        P(("expert", "cuts"), None),
        P(("expert", "cuts"), None),
        P(("expert", "cuts"), None),
        P(("expert", "cuts")),
        P(("expert", "cuts")),
        P(("expert", "cuts"), None),
        P(("expert", "cuts"), None),
        P(),
        P("cuts", None),
        P("expert", None),
        P("expert", None),
        P("expert", None, "cuts"),
        P("expert", None, "cuts"),
        P("expert", "cuts", None),
    )
    return jax.shard_map(
        on_device,
        mesh=mesh,
        in_specs=placed,
        out_specs=(P(("expert", "cuts"), None), P(("expert", "cuts"), None)),
        check_vma=False,
    )
```

```python
import math

import jax
import jax.numpy as jnp
from jax import lax
from jax.sharding import PartitionSpec as P

HEADS = 16
HEAD = 128
TOPK = 4
TREE = 64
CAP = 8
N_CHUNKS = 2


epsilon = 1e-06


def ancestors(parents):
    slot_ids = jnp.arange(TREE, dtype=jnp.int32)
    linked = (parents[:, None] == slot_ids[None, :]) | (slot_ids[:, None] == slot_ids[None, :])
    reach = linked.astype(jnp.float32)
    for doubling in range(TREE.bit_length()):
        reach = jnp.minimum(jnp.dot(reach, reach, precision=lax.Precision.HIGHEST), 1.0)
    return reach > 0.5


def tree_attention(request):
    queries, new_keys, new_values, cache_keys, cache_values, parents, tree_len, cache_len = request
    cache_rows = cache_keys.shape[0]
    query_heads = queries.reshape(TREE, HEADS, HEAD)
    cache_heads = cache_keys.reshape(cache_rows, HEADS, HEAD)
    fresh_heads = new_keys.reshape(TREE, HEADS, HEAD)
    score_scale = 1.0 / math.sqrt(HEAD)
    cache_scores = (
        jnp.einsum("qhd,khd->hqk", query_heads, cache_heads, preferred_element_type=jnp.float32)
        * score_scale
    )
    fresh_scores = (
        jnp.einsum("qhd,khd->hqk", query_heads, fresh_heads, preferred_element_type=jnp.float32)
        * score_scale
    )
    slot_ids = jnp.arange(TREE, dtype=jnp.int32)
    cache_seen = jnp.arange(cache_rows, dtype=jnp.int32) < cache_len
    fresh_seen = ancestors(parents) & (slot_ids[None, :] < tree_len)
    cache_scores = jnp.where(cache_seen[None, None, :], cache_scores, -jnp.inf)
    fresh_scores = jnp.where(fresh_seen[None, :, :], fresh_scores, -jnp.inf)
    highest = jnp.maximum(jnp.max(cache_scores, axis=2), jnp.max(fresh_scores, axis=2))[:, :, None]
    cache_exp = jnp.exp(cache_scores - highest)
    fresh_exp = jnp.exp(fresh_scores - highest)
    total = jnp.sum(cache_exp, axis=2, keepdims=True) + jnp.sum(fresh_exp, axis=2, keepdims=True)
    cache_weights = (cache_exp / total).astype(jnp.bfloat16)
    fresh_weights = (fresh_exp / total).astype(jnp.bfloat16)
    mixed = jnp.einsum(
        "hqk,khd->qhd",
        cache_weights,
        cache_values.reshape(cache_rows, HEADS, HEAD),
        preferred_element_type=jnp.float32,
    )
    mixed = mixed + jnp.einsum(
        "hqk,khd->qhd",
        fresh_weights,
        new_values.reshape(TREE, HEADS, HEAD),
        preferred_element_type=jnp.float32,
    )
    return mixed.reshape(TREE, HEADS * HEAD).astype(jnp.bfloat16)


def expert_rows(flat_in, gate_w, up_w, down_w):
    gate = jnp.dot(flat_in, gate_w, preferred_element_type=jnp.float32)
    upper = jnp.dot(flat_in, up_w, preferred_element_type=jnp.float32)
    hidden = (jax.nn.silu(gate) * upper).astype(jnp.bfloat16)
    return jnp.dot(hidden, down_w, preferred_element_type=jnp.float32)


def norm_rows(stream, norm_gain):
    power = jnp.mean(stream * stream, axis=1, keepdims=True)
    return (stream * lax.rsqrt(power + epsilon) * norm_gain).astype(jnp.bfloat16)


def on_device(
    queries,
    new_keys,
    new_values,
    cache_keys,
    cache_values,
    parents,
    tree_len,
    cache_len,
    accepted_path,
    residual,
    norm_gain,
    out_weight,
    routes,
    route_weights,
    w_gate,
    w_up,
    w_down,
):
    place = lax.axis_index("cuts")
    tok_rows = queries.shape[0]
    requests = tok_rows // TREE
    cache_rows = cache_keys.shape[0] // requests
    width = queries.shape[1]
    attended = lax.map(
        tree_attention,
        (
            queries.reshape(requests, TREE, width),
            new_keys.reshape(requests, TREE, width),
            new_values.reshape(requests, TREE, width),
            cache_keys.reshape(requests, cache_rows, width),
            cache_values.reshape(requests, cache_rows, width),
            parents,
            tree_len,
            cache_len,
        ),
    )
    attended = attended.reshape(tok_rows, width)
    head_group = lax.all_to_all(attended, "cuts", split_axis=1, concat_axis=0, tiled=True)
    gate_full = lax.all_gather(w_gate[0], "cuts", axis=0)
    up_full = lax.all_gather(w_up[0], "cuts", axis=0)
    cut_count = lax.axis_size("cuts")
    down_parts = [w_down[0]] + [
        lax.ppermute(w_down[0], "cuts", [(i, (i + shift) % cut_count) for i in range(cut_count)])
        for shift in range(1, cut_count)
    ]
    projected = jnp.dot(head_group, out_weight, preferred_element_type=jnp.float32)
    partials = lax.all_to_all(
        projected.astype(jnp.bfloat16).reshape(lax.axis_size("cuts"), tok_rows, width),
        "cuts",
        split_axis=0,
        concat_axis=0,
        tiled=True,
    )
    stream = residual.astype(jnp.float32) + jnp.sum(partials.astype(jnp.float32), axis=0)
    normed = norm_rows(stream, norm_gain)

    experts_all = w_gate.shape[0] * lax.axis_size("expert")
    capacity = CAP
    start = place * tok_rows
    own_routes = lax.dynamic_slice_in_dim(routes, start, tok_rows, 0)
    own_gains = lax.dynamic_slice_in_dim(route_weights, start, tok_rows, 0)
    flat = own_routes.reshape(tok_rows * TOPK)
    onehot = (flat[:, None] == jnp.arange(experts_all, dtype=jnp.int32)[None, :]).astype(jnp.int32)
    ahead = jnp.cumsum(onehot, axis=0) - onehot
    slot_of = jnp.sum(ahead * onehot, axis=1)
    dest = flat * capacity + slot_of
    token_of = jnp.arange(tok_rows * TOPK, dtype=jnp.int32) // TOPK
    table = jnp.full((experts_all * capacity,), -1, jnp.int32).at[dest].set(token_of)
    filled = table >= 0
    outgoing = jnp.where(
        filled[:, None], normed[jnp.maximum(table, 0)], jnp.zeros((), jnp.bfloat16)
    )
    outgoing = outgoing.reshape(experts_all, capacity, width)
    arrived = lax.all_to_all(outgoing, "expert", split_axis=0, concat_axis=0, tiled=True)
    rows = arrived.reshape(-1, width)
    gate = jnp.einsum("rd,cdf->rcf", rows, gate_full, preferred_element_type=jnp.float32)
    upper = jnp.einsum("rd,cdf->rcf", rows, up_full, preferred_element_type=jnp.float32)
    hidden = (jax.nn.silu(gate) * upper).astype(jnp.bfloat16)
    product = None
    for shift, down_part in enumerate(down_parts):
        owner = (place - shift) % cut_count
        slice_hidden = lax.dynamic_index_in_dim(hidden, owner, axis=1, keepdims=False)
        term = jnp.dot(slice_hidden, down_part, preferred_element_type=jnp.float32)
        product = term if product is None else product + term
    returned = lax.all_to_all(
        product.astype(jnp.bfloat16).reshape(experts_all, capacity, width),
        "expert",
        split_axis=0,
        concat_axis=0,
        tiled=True,
    )
    picked = returned.reshape(-1, width)[dest].reshape(tok_rows, TOPK, width)
    moe = jnp.sum(own_gains[:, :, None] * picked.astype(jnp.float32), axis=1)
    layer_out = (stream + moe).astype(jnp.bfloat16)
    picks = (jnp.arange(requests, dtype=jnp.int32)[:, None] * TREE + accepted_path).reshape(-1)
    accepted_kv = jnp.concatenate([new_keys[picks], new_values[picks]], axis=1)
    return (layer_out, accepted_kv)


def solution(mesh):
    placed = (
        P(("expert", "cuts"), None),
        P(("expert", "cuts"), None),
        P(("expert", "cuts"), None),
        P(("expert", "cuts"), None),
        P(("expert", "cuts"), None),
        P(("expert", "cuts"), None),
        P(("expert", "cuts")),
        P(("expert", "cuts")),
        P(("expert", "cuts"), None),
        P(("expert", "cuts"), None),
        P(),
        P("cuts", None),
        P("expert", None),
        P("expert", None),
        P("expert", None, "cuts"),
        P("expert", None, "cuts"),
        P("expert", "cuts", None),
    )
    return jax.shard_map(
        on_device,
        mesh=mesh,
        in_specs=placed,
        out_specs=(P(("expert", "cuts"), None), P(("expert", "cuts"), None)),
        check_vma=False,
    )
```

```python
import math

import jax
import jax.numpy as jnp
from jax import lax
from jax.sharding import PartitionSpec as P

HEADS = 16
HEAD = 128
TOPK = 4
TREE = 64
CAP = 8
N_CHUNKS = 2


epsilon = 1e-06


def ancestors(parents):
    slot_ids = jnp.arange(TREE, dtype=jnp.int32)
    linked = (parents[:, None] == slot_ids[None, :]) | (slot_ids[:, None] == slot_ids[None, :])
    reach = linked.astype(jnp.float32)
    for doubling in range(TREE.bit_length()):
        reach = jnp.minimum(jnp.dot(reach, reach, precision=lax.Precision.HIGHEST), 1.0)
    return reach > 0.5


def tree_attention(request):
    queries, new_keys, new_values, cache_keys, cache_values, parents, tree_len, cache_len = request
    cache_rows = cache_keys.shape[0]
    query_heads = queries.reshape(TREE, HEADS, HEAD)
    cache_heads = cache_keys.reshape(cache_rows, HEADS, HEAD)
    fresh_heads = new_keys.reshape(TREE, HEADS, HEAD)
    score_scale = 1.0 / math.sqrt(HEAD)
    cache_scores = (
        jnp.einsum("qhd,khd->hqk", query_heads, cache_heads, preferred_element_type=jnp.float32)
        * score_scale
    )
    fresh_scores = (
        jnp.einsum("qhd,khd->hqk", query_heads, fresh_heads, preferred_element_type=jnp.float32)
        * score_scale
    )
    slot_ids = jnp.arange(TREE, dtype=jnp.int32)
    cache_seen = jnp.arange(cache_rows, dtype=jnp.int32) < cache_len
    fresh_seen = ancestors(parents) & (slot_ids[None, :] < tree_len)
    cache_scores = jnp.where(cache_seen[None, None, :], cache_scores, -jnp.inf)
    fresh_scores = jnp.where(fresh_seen[None, :, :], fresh_scores, -jnp.inf)
    highest = jnp.maximum(jnp.max(cache_scores, axis=2), jnp.max(fresh_scores, axis=2))[:, :, None]
    cache_exp = jnp.exp(cache_scores - highest)
    fresh_exp = jnp.exp(fresh_scores - highest)
    total = jnp.sum(cache_exp, axis=2, keepdims=True) + jnp.sum(fresh_exp, axis=2, keepdims=True)
    cache_weights = (cache_exp / total).astype(jnp.bfloat16)
    fresh_weights = (fresh_exp / total).astype(jnp.bfloat16)
    mixed = jnp.einsum(
        "hqk,khd->qhd",
        cache_weights,
        cache_values.reshape(cache_rows, HEADS, HEAD),
        preferred_element_type=jnp.float32,
    )
    mixed = mixed + jnp.einsum(
        "hqk,khd->qhd",
        fresh_weights,
        new_values.reshape(TREE, HEADS, HEAD),
        preferred_element_type=jnp.float32,
    )
    return mixed.reshape(TREE, HEADS * HEAD).astype(jnp.bfloat16)


def expert_rows(flat_in, gate_w, up_w, down_w):
    gate = jnp.dot(flat_in, gate_w, preferred_element_type=jnp.float32)
    upper = jnp.dot(flat_in, up_w, preferred_element_type=jnp.float32)
    hidden = (jax.nn.silu(gate) * upper).astype(jnp.bfloat16)
    return jnp.dot(hidden, down_w, preferred_element_type=jnp.float32)


def norm_rows(stream, norm_gain):
    power = jnp.mean(stream * stream, axis=1, keepdims=True)
    return (stream * lax.rsqrt(power + epsilon) * norm_gain).astype(jnp.bfloat16)


def on_device(
    queries,
    new_keys,
    new_values,
    cache_keys,
    cache_values,
    parents,
    tree_len,
    cache_len,
    accepted_path,
    residual,
    norm_gain,
    out_weight,
    routes,
    route_weights,
    w_gate,
    w_up,
    w_down,
):
    place = lax.axis_index("cuts")
    tok_rows = queries.shape[0]
    requests = tok_rows // TREE
    cache_rows = cache_keys.shape[0] // requests
    width = queries.shape[1]
    attended = lax.map(
        tree_attention,
        (
            queries.reshape(requests, TREE, width),
            new_keys.reshape(requests, TREE, width),
            new_values.reshape(requests, TREE, width),
            cache_keys.reshape(requests, cache_rows, width),
            cache_values.reshape(requests, cache_rows, width),
            parents,
            tree_len,
            cache_len,
        ),
    )
    attended = attended.reshape(tok_rows, width)
    head_group = lax.all_to_all(attended, "cuts", split_axis=1, concat_axis=0, tiled=True)
    gate_full = lax.all_gather(w_gate[0], "cuts", axis=0)
    up_full = lax.all_gather(w_up[0], "cuts", axis=0)
    cut_count = lax.axis_size("cuts")
    half = width // 2
    down_early = w_down[0][:, :half]
    down_parts = [down_early] + [
        lax.ppermute(down_early, "cuts", [(i, (i + shift) % cut_count) for i in range(cut_count)])
        for shift in range(1, cut_count)
    ]
    down_late = lax.all_gather(w_down[0][:, half:], "cuts", axis=0)
    projected = jnp.dot(head_group, out_weight, preferred_element_type=jnp.float32)
    partials = lax.all_to_all(
        projected.astype(jnp.bfloat16).reshape(lax.axis_size("cuts"), tok_rows, width),
        "cuts",
        split_axis=0,
        concat_axis=0,
        tiled=True,
    )
    stream = residual.astype(jnp.float32) + jnp.sum(partials.astype(jnp.float32), axis=0)
    normed = norm_rows(stream, norm_gain)

    experts_all = w_gate.shape[0] * lax.axis_size("expert")
    capacity = CAP
    start = place * tok_rows
    own_routes = lax.dynamic_slice_in_dim(routes, start, tok_rows, 0)
    own_gains = lax.dynamic_slice_in_dim(route_weights, start, tok_rows, 0)
    flat = own_routes.reshape(tok_rows * TOPK)
    onehot = (flat[:, None] == jnp.arange(experts_all, dtype=jnp.int32)[None, :]).astype(jnp.int32)
    ahead = jnp.cumsum(onehot, axis=0) - onehot
    slot_of = jnp.sum(ahead * onehot, axis=1)
    dest = flat * capacity + slot_of
    token_of = jnp.arange(tok_rows * TOPK, dtype=jnp.int32) // TOPK
    table = jnp.full((experts_all * capacity,), -1, jnp.int32).at[dest].set(token_of)
    filled = table >= 0
    outgoing = jnp.where(
        filled[:, None], normed[jnp.maximum(table, 0)], jnp.zeros((), jnp.bfloat16)
    )
    outgoing = outgoing.reshape(experts_all, capacity, width)
    arrived = lax.all_to_all(outgoing, "expert", split_axis=0, concat_axis=0, tiled=True)
    rows = arrived.reshape(-1, width)
    gate = jnp.einsum("rd,cdf->rcf", rows, gate_full, preferred_element_type=jnp.float32)
    upper = jnp.einsum("rd,cdf->rcf", rows, up_full, preferred_element_type=jnp.float32)
    hidden = (jax.nn.silu(gate) * upper).astype(jnp.bfloat16)
    product = None
    for shift, down_part in enumerate(down_parts):
        owner = (place - shift) % cut_count
        slice_hidden = lax.dynamic_index_in_dim(hidden, owner, axis=1, keepdims=False)
        term = jnp.dot(slice_hidden, down_part, preferred_element_type=jnp.float32)
        product = term if product is None else product + term
    returned_early = lax.all_to_all(
        product.astype(jnp.bfloat16).reshape(experts_all, capacity, half),
        "expert",
        split_axis=0,
        concat_axis=0,
        tiled=True,
    )
    product_late = jnp.einsum("rcf,cfd->rd", hidden, down_late, preferred_element_type=jnp.float32)
    returned_late = lax.all_to_all(
        product_late.astype(jnp.bfloat16).reshape(experts_all, capacity, half),
        "expert",
        split_axis=0,
        concat_axis=0,
        tiled=True,
    )
    moe_parts = []
    for returned in (returned_early, returned_late):
        picked = returned.reshape(-1, half)[dest].reshape(tok_rows, TOPK, half)
        moe_parts.append(jnp.sum(own_gains[:, :, None] * picked.astype(jnp.float32), axis=1))
    moe = jnp.concatenate(moe_parts, axis=1)
    layer_out = (stream + moe).astype(jnp.bfloat16)
    picks = (jnp.arange(requests, dtype=jnp.int32)[:, None] * TREE + accepted_path).reshape(-1)
    accepted_kv = jnp.concatenate([new_keys[picks], new_values[picks]], axis=1)
    return (layer_out, accepted_kv)


def solution(mesh):
    placed = (
        P(("expert", "cuts"), None),
        P(("expert", "cuts"), None),
        P(("expert", "cuts"), None),
        P(("expert", "cuts"), None),
        P(("expert", "cuts"), None),
        P(("expert", "cuts"), None),
        P(("expert", "cuts")),
        P(("expert", "cuts")),
        P(("expert", "cuts"), None),
        P(("expert", "cuts"), None),
        P(),
        P("cuts", None),
        P("expert", None),
        P("expert", None),
        P("expert", None, "cuts"),
        P("expert", None, "cuts"),
        P("expert", "cuts", None),
    )
    return jax.shard_map(
        on_device,
        mesh=mesh,
        in_specs=placed,
        out_specs=(P(("expert", "cuts"), None), P(("expert", "cuts"), None)),
        check_vma=False,
    )
```

```python
import math

import jax
import jax.numpy as jnp
from jax import lax
from jax.sharding import PartitionSpec as P

HEADS = 16
HEAD = 128
TOPK = 4
TREE = 64
CAP = 8
N_CHUNKS = 2


epsilon = 1e-06


def ancestors(parents):
    slot_ids = jnp.arange(TREE, dtype=jnp.int32)
    linked = (parents[:, None] == slot_ids[None, :]) | (slot_ids[:, None] == slot_ids[None, :])
    reach = linked.astype(jnp.float32)
    for doubling in range(TREE.bit_length()):
        reach = jnp.minimum(jnp.dot(reach, reach, precision=lax.Precision.HIGHEST), 1.0)
    return reach > 0.5


def tree_attention(request):
    queries, new_keys, new_values, cache_keys, cache_values, parents, tree_len, cache_len = request
    cache_rows = cache_keys.shape[0]
    query_heads = queries.reshape(TREE, HEADS, HEAD)
    cache_heads = cache_keys.reshape(cache_rows, HEADS, HEAD)
    fresh_heads = new_keys.reshape(TREE, HEADS, HEAD)
    score_scale = 1.0 / math.sqrt(HEAD)
    cache_scores = (
        jnp.einsum("qhd,khd->hqk", query_heads, cache_heads, preferred_element_type=jnp.float32)
        * score_scale
    )
    fresh_scores = (
        jnp.einsum("qhd,khd->hqk", query_heads, fresh_heads, preferred_element_type=jnp.float32)
        * score_scale
    )
    slot_ids = jnp.arange(TREE, dtype=jnp.int32)
    cache_seen = jnp.arange(cache_rows, dtype=jnp.int32) < cache_len
    fresh_seen = ancestors(parents) & (slot_ids[None, :] < tree_len)
    cache_scores = jnp.where(cache_seen[None, None, :], cache_scores, -jnp.inf)
    fresh_scores = jnp.where(fresh_seen[None, :, :], fresh_scores, -jnp.inf)
    highest = jnp.maximum(jnp.max(cache_scores, axis=2), jnp.max(fresh_scores, axis=2))[:, :, None]
    cache_exp = jnp.exp(cache_scores - highest)
    fresh_exp = jnp.exp(fresh_scores - highest)
    total = jnp.sum(cache_exp, axis=2, keepdims=True) + jnp.sum(fresh_exp, axis=2, keepdims=True)
    cache_weights = (cache_exp / total).astype(jnp.bfloat16)
    fresh_weights = (fresh_exp / total).astype(jnp.bfloat16)
    mixed = jnp.einsum(
        "hqk,khd->qhd",
        cache_weights,
        cache_values.reshape(cache_rows, HEADS, HEAD),
        preferred_element_type=jnp.float32,
    )
    mixed = mixed + jnp.einsum(
        "hqk,khd->qhd",
        fresh_weights,
        new_values.reshape(TREE, HEADS, HEAD),
        preferred_element_type=jnp.float32,
    )
    return mixed.reshape(TREE, HEADS * HEAD).astype(jnp.bfloat16)


def expert_rows(flat_in, gate_w, up_w, down_w):
    gate = jnp.dot(flat_in, gate_w, preferred_element_type=jnp.float32)
    upper = jnp.dot(flat_in, up_w, preferred_element_type=jnp.float32)
    hidden = (jax.nn.silu(gate) * upper).astype(jnp.bfloat16)
    return jnp.dot(hidden, down_w, preferred_element_type=jnp.float32)


def norm_rows(stream, norm_gain):
    power = jnp.mean(stream * stream, axis=1, keepdims=True)
    return (stream * lax.rsqrt(power + epsilon) * norm_gain).astype(jnp.bfloat16)


def on_device(
    queries,
    new_keys,
    new_values,
    cache_keys,
    cache_values,
    parents,
    tree_len,
    cache_len,
    accepted_path,
    residual,
    norm_gain,
    out_weight,
    routes,
    route_weights,
    w_gate,
    w_up,
    w_down,
):
    place = lax.axis_index("cuts")
    tok_rows = queries.shape[0]
    requests = tok_rows // TREE
    cache_rows = cache_keys.shape[0] // requests
    width = queries.shape[1]
    attended = lax.map(
        tree_attention,
        (
            queries.reshape(requests, TREE, width),
            new_keys.reshape(requests, TREE, width),
            new_values.reshape(requests, TREE, width),
            cache_keys.reshape(requests, cache_rows, width),
            cache_values.reshape(requests, cache_rows, width),
            parents,
            tree_len,
            cache_len,
        ),
    )
    attended = attended.reshape(tok_rows, width)
    head_group = lax.all_to_all(attended, "cuts", split_axis=1, concat_axis=0, tiled=True)
    gate_up_full = lax.all_gather(jnp.stack([w_gate[0], w_up[0]]), "cuts", axis=0)
    cut_count = lax.axis_size("cuts")
    half = width // 2
    down_early = w_down[0][:, :half]
    down_parts = [down_early] + [
        lax.ppermute(down_early, "cuts", [(i, (i + shift) % cut_count) for i in range(cut_count)])
        for shift in range(1, cut_count)
    ]
    down_late = lax.all_gather(w_down[0][:, half:], "cuts", axis=0)
    projected = jnp.dot(head_group, out_weight, preferred_element_type=jnp.float32)
    partials = lax.all_to_all(
        projected.astype(jnp.bfloat16).reshape(lax.axis_size("cuts"), tok_rows, width),
        "cuts",
        split_axis=0,
        concat_axis=0,
        tiled=True,
    )
    stream = residual.astype(jnp.float32) + jnp.sum(partials.astype(jnp.float32), axis=0)
    normed = norm_rows(stream, norm_gain)

    experts_all = w_gate.shape[0] * lax.axis_size("expert")
    capacity = CAP
    start = place * tok_rows
    own_routes = lax.dynamic_slice_in_dim(routes, start, tok_rows, 0)
    own_gains = lax.dynamic_slice_in_dim(route_weights, start, tok_rows, 0)
    flat = own_routes.reshape(tok_rows * TOPK)
    onehot = (flat[:, None] == jnp.arange(experts_all, dtype=jnp.int32)[None, :]).astype(jnp.int32)
    ahead = jnp.cumsum(onehot, axis=0) - onehot
    slot_of = jnp.sum(ahead * onehot, axis=1)
    dest = flat * capacity + slot_of
    token_of = jnp.arange(tok_rows * TOPK, dtype=jnp.int32) // TOPK
    table = jnp.full((experts_all * capacity,), -1, jnp.int32).at[dest].set(token_of)
    filled = table >= 0
    outgoing = jnp.where(
        filled[:, None], normed[jnp.maximum(table, 0)], jnp.zeros((), jnp.bfloat16)
    )
    outgoing = outgoing.reshape(experts_all, capacity, width)
    arrived = lax.all_to_all(outgoing, "expert", split_axis=0, concat_axis=0, tiled=True)
    rows = arrived.reshape(-1, width)
    gate = jnp.einsum("rd,cdf->rcf", rows, gate_up_full[:, 0], preferred_element_type=jnp.float32)
    upper = jnp.einsum("rd,cdf->rcf", rows, gate_up_full[:, 1], preferred_element_type=jnp.float32)
    hidden = (jax.nn.silu(gate) * upper).astype(jnp.bfloat16)
    product = None
    for shift, down_part in enumerate(down_parts):
        owner = (place - shift) % cut_count
        slice_hidden = lax.dynamic_index_in_dim(hidden, owner, axis=1, keepdims=False)
        term = jnp.dot(slice_hidden, down_part, preferred_element_type=jnp.float32)
        product = term if product is None else product + term
    returned_early = lax.all_to_all(
        product.astype(jnp.bfloat16).reshape(experts_all, capacity, half),
        "expert",
        split_axis=0,
        concat_axis=0,
        tiled=True,
    )
    product_late = jnp.einsum("rcf,cfd->rd", hidden, down_late, preferred_element_type=jnp.float32)
    returned_late = lax.all_to_all(
        product_late.astype(jnp.bfloat16).reshape(experts_all, capacity, half),
        "expert",
        split_axis=0,
        concat_axis=0,
        tiled=True,
    )
    moe_parts = []
    for returned in (returned_early, returned_late):
        picked = returned.reshape(-1, half)[dest].reshape(tok_rows, TOPK, half)
        moe_parts.append(jnp.sum(own_gains[:, :, None] * picked.astype(jnp.float32), axis=1))
    moe = jnp.concatenate(moe_parts, axis=1)
    layer_out = (stream + moe).astype(jnp.bfloat16)
    picks = (jnp.arange(requests, dtype=jnp.int32)[:, None] * TREE + accepted_path).reshape(-1)
    accepted_kv = jnp.concatenate([new_keys[picks], new_values[picks]], axis=1)
    return (layer_out, accepted_kv)


def solution(mesh):
    placed = (
        P(("expert", "cuts"), None),
        P(("expert", "cuts"), None),
        P(("expert", "cuts"), None),
        P(("expert", "cuts"), None),
        P(("expert", "cuts"), None),
        P(("expert", "cuts"), None),
        P(("expert", "cuts")),
        P(("expert", "cuts")),
        P(("expert", "cuts"), None),
        P(("expert", "cuts"), None),
        P(),
        P("cuts", None),
        P("expert", None),
        P("expert", None),
        P("expert", None, "cuts"),
        P("expert", None, "cuts"),
        P("expert", "cuts", None),
    )
    return jax.shard_map(
        on_device,
        mesh=mesh,
        in_specs=placed,
        out_specs=(P(("expert", "cuts"), None), P(("expert", "cuts"), None)),
        check_vma=False,
    )
```

```python
import math

import jax
import jax.numpy as jnp
from jax import lax
from jax.sharding import PartitionSpec as P

HEADS = 16
HEAD = 128
TOPK = 4
TREE = 64
CAP = 8
N_CHUNKS = 2


epsilon = 1e-06


def ancestors(parents):
    slot_ids = jnp.arange(TREE, dtype=jnp.int32)
    linked = (parents[:, None] == slot_ids[None, :]) | (slot_ids[:, None] == slot_ids[None, :])
    reach = linked.astype(jnp.float32)
    for doubling in range(TREE.bit_length()):
        reach = jnp.minimum(jnp.dot(reach, reach, precision=lax.Precision.HIGHEST), 1.0)
    return reach > 0.5


def tree_attention(request):
    queries, new_keys, new_values, cache_keys, cache_values, parents, tree_len, cache_len = request
    cache_rows = cache_keys.shape[0]
    query_heads = queries.reshape(TREE, HEADS, HEAD)
    cache_heads = cache_keys.reshape(cache_rows, HEADS, HEAD)
    fresh_heads = new_keys.reshape(TREE, HEADS, HEAD)
    score_scale = 1.0 / math.sqrt(HEAD)
    cache_scores = (
        jnp.einsum("qhd,khd->hqk", query_heads, cache_heads, preferred_element_type=jnp.float32)
        * score_scale
    )
    fresh_scores = (
        jnp.einsum("qhd,khd->hqk", query_heads, fresh_heads, preferred_element_type=jnp.float32)
        * score_scale
    )
    slot_ids = jnp.arange(TREE, dtype=jnp.int32)
    cache_seen = jnp.arange(cache_rows, dtype=jnp.int32) < cache_len
    fresh_seen = ancestors(parents) & (slot_ids[None, :] < tree_len)
    cache_scores = jnp.where(cache_seen[None, None, :], cache_scores, -jnp.inf)
    fresh_scores = jnp.where(fresh_seen[None, :, :], fresh_scores, -jnp.inf)
    highest = jnp.maximum(jnp.max(cache_scores, axis=2), jnp.max(fresh_scores, axis=2))[:, :, None]
    cache_exp = jnp.exp(cache_scores - highest)
    fresh_exp = jnp.exp(fresh_scores - highest)
    total = jnp.sum(cache_exp, axis=2, keepdims=True) + jnp.sum(fresh_exp, axis=2, keepdims=True)
    cache_weights = (cache_exp / total).astype(jnp.bfloat16)
    fresh_weights = (fresh_exp / total).astype(jnp.bfloat16)
    mixed = jnp.einsum(
        "hqk,khd->qhd",
        cache_weights,
        cache_values.reshape(cache_rows, HEADS, HEAD),
        preferred_element_type=jnp.float32,
    )
    mixed = mixed + jnp.einsum(
        "hqk,khd->qhd",
        fresh_weights,
        new_values.reshape(TREE, HEADS, HEAD),
        preferred_element_type=jnp.float32,
    )
    return mixed.reshape(TREE, HEADS * HEAD).astype(jnp.bfloat16)


def expert_rows(flat_in, gate_w, up_w, down_w):
    gate = jnp.dot(flat_in, gate_w, preferred_element_type=jnp.float32)
    upper = jnp.dot(flat_in, up_w, preferred_element_type=jnp.float32)
    hidden = (jax.nn.silu(gate) * upper).astype(jnp.bfloat16)
    return jnp.dot(hidden, down_w, preferred_element_type=jnp.float32)


def norm_rows(stream, norm_gain):
    power = jnp.mean(stream * stream, axis=1, keepdims=True)
    return (stream * lax.rsqrt(power + epsilon) * norm_gain).astype(jnp.bfloat16)


def on_device(
    queries,
    new_keys,
    new_values,
    cache_keys,
    cache_values,
    parents,
    tree_len,
    cache_len,
    accepted_path,
    residual,
    norm_gain,
    out_weight,
    routes,
    route_weights,
    w_gate,
    w_up,
    w_down,
):
    place = lax.axis_index("cuts")
    tok_rows = queries.shape[0]
    requests = tok_rows // TREE
    cache_rows = cache_keys.shape[0] // requests
    width = queries.shape[1]
    attended = lax.map(
        tree_attention,
        (
            queries.reshape(requests, TREE, width),
            new_keys.reshape(requests, TREE, width),
            new_values.reshape(requests, TREE, width),
            cache_keys.reshape(requests, cache_rows, width),
            cache_values.reshape(requests, cache_rows, width),
            parents,
            tree_len,
            cache_len,
        ),
    )
    attended = attended.reshape(tok_rows, width)
    head_group = lax.all_to_all(attended, "cuts", split_axis=1, concat_axis=0, tiled=True)
    gate_full = lax.all_gather(w_gate[0], "cuts", axis=0)
    cut_count = lax.axis_size("cuts")
    half = width // 2
    down_early = w_down[0][:, :half]
    down_parts = [down_early] + [
        lax.ppermute(down_early, "cuts", [(i, (i + shift) % cut_count) for i in range(cut_count)])
        for shift in range(1, cut_count)
    ]
    down_late = lax.all_gather(w_down[0][:, half:], "cuts", axis=0)
    up_parts = [w_up[0]] + [
        lax.ppermute(w_up[0], "cuts", [(i, (i + shift) % cut_count) for i in range(cut_count)])
        for shift in range(1, cut_count)
    ]
    projected = jnp.dot(head_group, out_weight, preferred_element_type=jnp.float32)
    partials = lax.all_to_all(
        projected.astype(jnp.bfloat16).reshape(lax.axis_size("cuts"), tok_rows, width),
        "cuts",
        split_axis=0,
        concat_axis=0,
        tiled=True,
    )
    stream = residual.astype(jnp.float32) + jnp.sum(partials.astype(jnp.float32), axis=0)
    normed = norm_rows(stream, norm_gain)

    experts_all = w_gate.shape[0] * lax.axis_size("expert")
    capacity = CAP
    start = place * tok_rows
    own_routes = lax.dynamic_slice_in_dim(routes, start, tok_rows, 0)
    own_gains = lax.dynamic_slice_in_dim(route_weights, start, tok_rows, 0)
    flat = own_routes.reshape(tok_rows * TOPK)
    onehot = (flat[:, None] == jnp.arange(experts_all, dtype=jnp.int32)[None, :]).astype(jnp.int32)
    ahead = jnp.cumsum(onehot, axis=0) - onehot
    slot_of = jnp.sum(ahead * onehot, axis=1)
    dest = flat * capacity + slot_of
    token_of = jnp.arange(tok_rows * TOPK, dtype=jnp.int32) // TOPK
    table = jnp.full((experts_all * capacity,), -1, jnp.int32).at[dest].set(token_of)
    filled = table >= 0
    outgoing = jnp.where(
        filled[:, None], normed[jnp.maximum(table, 0)], jnp.zeros((), jnp.bfloat16)
    )
    outgoing = outgoing.reshape(experts_all, capacity, width)
    arrived = lax.all_to_all(outgoing, "expert", split_axis=0, concat_axis=0, tiled=True)
    rows = arrived.reshape(-1, width)
    gate = jnp.einsum("rd,cdf->rcf", rows, gate_full, preferred_element_type=jnp.float32)
    slices = []
    for shift, up_part in enumerate(up_parts):
        owner = (place - shift) % cut_count
        slice_gate = lax.dynamic_index_in_dim(gate, owner, axis=1, keepdims=False)
        upper = jnp.dot(rows, up_part, preferred_element_type=jnp.float32)
        slices.append((owner, (jax.nn.silu(slice_gate) * upper).astype(jnp.bfloat16)))
    product = None
    for (owner, slice_hidden), down_part in zip(slices, down_parts):
        term = jnp.dot(slice_hidden, down_part, preferred_element_type=jnp.float32)
        product = term if product is None else product + term
    returned_early = lax.all_to_all(
        product.astype(jnp.bfloat16).reshape(experts_all, capacity, half),
        "expert",
        split_axis=0,
        concat_axis=0,
        tiled=True,
    )
    product_late = None
    for owner, slice_hidden in slices:
        down_w = lax.dynamic_index_in_dim(down_late, owner, axis=0, keepdims=False)
        term = jnp.dot(slice_hidden, down_w, preferred_element_type=jnp.float32)
        product_late = term if product_late is None else product_late + term
    returned_late = lax.all_to_all(
        product_late.astype(jnp.bfloat16).reshape(experts_all, capacity, half),
        "expert",
        split_axis=0,
        concat_axis=0,
        tiled=True,
    )
    moe_parts = []
    for returned in (returned_early, returned_late):
        picked = returned.reshape(-1, half)[dest].reshape(tok_rows, TOPK, half)
        moe_parts.append(jnp.sum(own_gains[:, :, None] * picked.astype(jnp.float32), axis=1))
    moe = jnp.concatenate(moe_parts, axis=1)
    layer_out = (stream + moe).astype(jnp.bfloat16)
    picks = (jnp.arange(requests, dtype=jnp.int32)[:, None] * TREE + accepted_path).reshape(-1)
    accepted_kv = jnp.concatenate([new_keys[picks], new_values[picks]], axis=1)
    return (layer_out, accepted_kv)


def solution(mesh):
    placed = (
        P(("expert", "cuts"), None),
        P(("expert", "cuts"), None),
        P(("expert", "cuts"), None),
        P(("expert", "cuts"), None),
        P(("expert", "cuts"), None),
        P(("expert", "cuts"), None),
        P(("expert", "cuts")),
        P(("expert", "cuts")),
        P(("expert", "cuts"), None),
        P(("expert", "cuts"), None),
        P(),
        P("cuts", None),
        P("expert", None),
        P("expert", None),
        P("expert", None, "cuts"),
        P("expert", None, "cuts"),
        P("expert", "cuts", None),
    )
    return jax.shard_map(
        on_device,
        mesh=mesh,
        in_specs=placed,
        out_specs=(P(("expert", "cuts"), None), P(("expert", "cuts"), None)),
        check_vma=False,
    )
```

```python
import math

import jax
import jax.numpy as jnp
from jax import lax
from jax.sharding import PartitionSpec as P

HEADS = 16
HEAD = 128
TOPK = 4
TREE = 64
CAP = 8
N_CHUNKS = 2


epsilon = 1e-06


def ancestors(parents):
    slot_ids = jnp.arange(TREE, dtype=jnp.int32)
    linked = (parents[:, None] == slot_ids[None, :]) | (slot_ids[:, None] == slot_ids[None, :])
    reach = linked.astype(jnp.float32)
    for doubling in range(TREE.bit_length()):
        reach = jnp.minimum(jnp.dot(reach, reach, precision=lax.Precision.HIGHEST), 1.0)
    return reach > 0.5


def tree_attention(request):
    queries, new_keys, new_values, cache_keys, cache_values, parents, tree_len, cache_len = request
    cache_rows = cache_keys.shape[0]
    query_heads = queries.reshape(TREE, HEADS, HEAD)
    cache_heads = cache_keys.reshape(cache_rows, HEADS, HEAD)
    fresh_heads = new_keys.reshape(TREE, HEADS, HEAD)
    score_scale = 1.0 / math.sqrt(HEAD)
    cache_scores = (
        jnp.einsum("qhd,khd->hqk", query_heads, cache_heads, preferred_element_type=jnp.float32)
        * score_scale
    )
    fresh_scores = (
        jnp.einsum("qhd,khd->hqk", query_heads, fresh_heads, preferred_element_type=jnp.float32)
        * score_scale
    )
    slot_ids = jnp.arange(TREE, dtype=jnp.int32)
    cache_seen = jnp.arange(cache_rows, dtype=jnp.int32) < cache_len
    fresh_seen = ancestors(parents) & (slot_ids[None, :] < tree_len)
    cache_scores = jnp.where(cache_seen[None, None, :], cache_scores, -jnp.inf)
    fresh_scores = jnp.where(fresh_seen[None, :, :], fresh_scores, -jnp.inf)
    highest = jnp.maximum(jnp.max(cache_scores, axis=2), jnp.max(fresh_scores, axis=2))[:, :, None]
    cache_exp = jnp.exp(cache_scores - highest)
    fresh_exp = jnp.exp(fresh_scores - highest)
    total = jnp.sum(cache_exp, axis=2, keepdims=True) + jnp.sum(fresh_exp, axis=2, keepdims=True)
    cache_weights = (cache_exp / total).astype(jnp.bfloat16)
    fresh_weights = (fresh_exp / total).astype(jnp.bfloat16)
    mixed = jnp.einsum(
        "hqk,khd->qhd",
        cache_weights,
        cache_values.reshape(cache_rows, HEADS, HEAD),
        preferred_element_type=jnp.float32,
    )
    mixed = mixed + jnp.einsum(
        "hqk,khd->qhd",
        fresh_weights,
        new_values.reshape(TREE, HEADS, HEAD),
        preferred_element_type=jnp.float32,
    )
    return mixed.reshape(TREE, HEADS * HEAD).astype(jnp.bfloat16)


def expert_rows(flat_in, gate_w, up_w, down_w):
    gate = jnp.dot(flat_in, gate_w, preferred_element_type=jnp.float32)
    upper = jnp.dot(flat_in, up_w, preferred_element_type=jnp.float32)
    hidden = (jax.nn.silu(gate) * upper).astype(jnp.bfloat16)
    return jnp.dot(hidden, down_w, preferred_element_type=jnp.float32)


def norm_rows(stream, norm_gain):
    power = jnp.mean(stream * stream, axis=1, keepdims=True)
    return (stream * lax.rsqrt(power + epsilon) * norm_gain).astype(jnp.bfloat16)


def on_device(
    queries,
    new_keys,
    new_values,
    cache_keys,
    cache_values,
    parents,
    tree_len,
    cache_len,
    accepted_path,
    residual,
    norm_gain,
    out_weight,
    routes,
    route_weights,
    w_gate,
    w_up,
    w_down,
):
    place = lax.axis_index("cuts")
    tok_rows = queries.shape[0]
    requests = tok_rows // TREE
    cache_rows = cache_keys.shape[0] // requests
    width = queries.shape[1]
    attended = lax.map(
        tree_attention,
        (
            queries.reshape(requests, TREE, width),
            new_keys.reshape(requests, TREE, width),
            new_values.reshape(requests, TREE, width),
            cache_keys.reshape(requests, cache_rows, width),
            cache_values.reshape(requests, cache_rows, width),
            parents,
            tree_len,
            cache_len,
        ),
    )
    attended = attended.reshape(tok_rows, width)
    head_group = lax.all_to_all(attended, "cuts", split_axis=1, concat_axis=0, tiled=True)
    gate_full = lax.all_gather(w_gate[0], "cuts", axis=0)
    up_full = lax.all_gather(w_up[0], "cuts", axis=0)
    cut_count = lax.axis_size("cuts")
    half = width // 2
    down_early = w_down[0][:, :half]
    down_parts = [down_early] + [
        lax.ppermute(down_early, "cuts", [(i, (i + shift) % cut_count) for i in range(cut_count)])
        for shift in range(1, cut_count)
    ]
    down_late = lax.all_gather(w_down[0][:, half:], "cuts", axis=0)
    projected = jnp.dot(head_group, out_weight, preferred_element_type=jnp.float32)
    partials = lax.all_to_all(
        projected.astype(jnp.bfloat16).reshape(lax.axis_size("cuts"), tok_rows, width),
        "cuts",
        split_axis=0,
        concat_axis=0,
        tiled=True,
    )
    stream = residual.astype(jnp.float32) + jnp.sum(partials.astype(jnp.float32), axis=0)
    normed = norm_rows(stream, norm_gain)

    experts_all = w_gate.shape[0] * lax.axis_size("expert")
    capacity = CAP
    start = place * tok_rows
    own_routes = lax.dynamic_slice_in_dim(routes, start, tok_rows, 0)
    own_gains = lax.dynamic_slice_in_dim(route_weights, start, tok_rows, 0)
    flat = own_routes.reshape(tok_rows * TOPK)
    onehot = (flat[:, None] == jnp.arange(experts_all, dtype=jnp.int32)[None, :]).astype(jnp.int32)
    ahead = jnp.cumsum(onehot, axis=0) - onehot
    slot_of = jnp.sum(ahead * onehot, axis=1)
    dest = flat * capacity + slot_of
    token_of = jnp.arange(tok_rows * TOPK, dtype=jnp.int32) // TOPK
    table = jnp.full((experts_all * capacity,), -1, jnp.int32).at[dest].set(token_of)
    filled = table >= 0
    outgoing = jnp.where(
        filled[:, None], normed[jnp.maximum(table, 0)], jnp.zeros((), jnp.bfloat16)
    )
    outgoing = outgoing.reshape(experts_all, capacity, width)
    arrived = lax.all_to_all(outgoing, "expert", split_axis=0, concat_axis=0, tiled=True)
    rows = arrived.reshape(-1, width)
    gate = jnp.einsum("rd,cdf->rcf", rows, gate_full, preferred_element_type=jnp.float32)
    upper = jnp.einsum("rd,cdf->rcf", rows, up_full, preferred_element_type=jnp.float32)
    hidden = (jax.nn.silu(gate) * upper).astype(jnp.bfloat16)
    product = None
    for shift, down_part in enumerate(down_parts):
        owner = (place - shift) % cut_count
        slice_hidden = lax.dynamic_index_in_dim(hidden, owner, axis=1, keepdims=False)
        term = jnp.dot(slice_hidden, down_part, preferred_element_type=jnp.float32)
        product = term if product is None else product + term
    returned_early = lax.all_to_all(
        product.astype(jnp.bfloat16).reshape(experts_all, capacity, half),
        "expert",
        split_axis=0,
        concat_axis=0,
        tiled=True,
    )
    product_late = jnp.einsum("rcf,cfd->rd", hidden, down_late, preferred_element_type=jnp.float32)
    returned_late = lax.all_to_all(
        product_late.astype(jnp.bfloat16).reshape(experts_all, capacity, half),
        "expert",
        split_axis=0,
        concat_axis=0,
        tiled=True,
    )
    route_major = dest.reshape(tok_rows, TOPK).T.reshape(-1)
    gains_route_major = own_gains.T[:, :, None]
    moe_parts = []
    for returned in (returned_early, returned_late):
        picked = returned.reshape(-1, half)[route_major].reshape(TOPK, tok_rows, half)
        moe_parts.append(jnp.sum(gains_route_major * picked.astype(jnp.float32), axis=0))
    moe = jnp.concatenate(moe_parts, axis=1)
    layer_out = (stream + moe).astype(jnp.bfloat16)
    picks = (jnp.arange(requests, dtype=jnp.int32)[:, None] * TREE + accepted_path).reshape(-1)
    accepted_kv = jnp.concatenate([new_keys[picks], new_values[picks]], axis=1)
    return (layer_out, accepted_kv)


def solution(mesh):
    placed = (
        P(("expert", "cuts"), None),
        P(("expert", "cuts"), None),
        P(("expert", "cuts"), None),
        P(("expert", "cuts"), None),
        P(("expert", "cuts"), None),
        P(("expert", "cuts"), None),
        P(("expert", "cuts")),
        P(("expert", "cuts")),
        P(("expert", "cuts"), None),
        P(("expert", "cuts"), None),
        P(),
        P("cuts", None),
        P("expert", None),
        P("expert", None),
        P("expert", None, "cuts"),
        P("expert", None, "cuts"),
        P("expert", "cuts", None),
    )
    return jax.shard_map(
        on_device,
        mesh=mesh,
        in_specs=placed,
        out_specs=(P(("expert", "cuts"), None), P(("expert", "cuts"), None)),
        check_vma=False,
    )
```

```python
import math

import jax
import jax.numpy as jnp
from jax import lax
from jax.sharding import PartitionSpec as P

HEADS = 16
HEAD = 128
TOPK = 4
TREE = 64
CAP = 8
N_CHUNKS = 2


epsilon = 1e-06


def ancestors(parents):
    slot_ids = jnp.arange(TREE, dtype=jnp.int32)
    linked = (parents[:, None] == slot_ids[None, :]) | (slot_ids[:, None] == slot_ids[None, :])
    reach = linked.astype(jnp.float32)
    for doubling in range(TREE.bit_length()):
        reach = jnp.minimum(jnp.dot(reach, reach, precision=lax.Precision.HIGHEST), 1.0)
    return reach > 0.5


def tree_attention(request):
    queries, new_keys, new_values, cache_keys, cache_values, parents, tree_len, cache_len = request
    cache_rows = cache_keys.shape[0]
    query_heads = queries.reshape(TREE, HEADS, HEAD)
    cache_heads = cache_keys.reshape(cache_rows, HEADS, HEAD)
    fresh_heads = new_keys.reshape(TREE, HEADS, HEAD)
    score_scale = 1.0 / math.sqrt(HEAD)
    cache_scores = (
        jnp.einsum("qhd,khd->hqk", query_heads, cache_heads, preferred_element_type=jnp.float32)
        * score_scale
    )
    fresh_scores = (
        jnp.einsum("qhd,khd->hqk", query_heads, fresh_heads, preferred_element_type=jnp.float32)
        * score_scale
    )
    slot_ids = jnp.arange(TREE, dtype=jnp.int32)
    cache_seen = jnp.arange(cache_rows, dtype=jnp.int32) < cache_len
    fresh_seen = ancestors(parents) & (slot_ids[None, :] < tree_len)
    cache_scores = jnp.where(cache_seen[None, None, :], cache_scores, -jnp.inf)
    fresh_scores = jnp.where(fresh_seen[None, :, :], fresh_scores, -jnp.inf)
    highest = jnp.maximum(jnp.max(cache_scores, axis=2), jnp.max(fresh_scores, axis=2))[:, :, None]
    cache_exp = jnp.exp(cache_scores - highest)
    fresh_exp = jnp.exp(fresh_scores - highest)
    total = jnp.sum(cache_exp, axis=2, keepdims=True) + jnp.sum(fresh_exp, axis=2, keepdims=True)
    cache_weights = (cache_exp / total).astype(jnp.bfloat16)
    fresh_weights = (fresh_exp / total).astype(jnp.bfloat16)
    mixed = jnp.einsum(
        "hqk,khd->qhd",
        cache_weights,
        cache_values.reshape(cache_rows, HEADS, HEAD),
        preferred_element_type=jnp.float32,
    )
    mixed = mixed + jnp.einsum(
        "hqk,khd->qhd",
        fresh_weights,
        new_values.reshape(TREE, HEADS, HEAD),
        preferred_element_type=jnp.float32,
    )
    return mixed.reshape(TREE, HEADS * HEAD).astype(jnp.bfloat16)


def expert_rows(flat_in, gate_w, up_w, down_w):
    gate = jnp.dot(flat_in, gate_w, preferred_element_type=jnp.float32)
    upper = jnp.dot(flat_in, up_w, preferred_element_type=jnp.float32)
    hidden = (jax.nn.silu(gate) * upper).astype(jnp.bfloat16)
    return jnp.dot(hidden, down_w, preferred_element_type=jnp.float32)


def norm_rows(stream, norm_gain):
    power = jnp.mean(stream * stream, axis=1, keepdims=True)
    return (stream * lax.rsqrt(power + epsilon) * norm_gain).astype(jnp.bfloat16)


def on_device(
    queries,
    new_keys,
    new_values,
    cache_keys,
    cache_values,
    parents,
    tree_len,
    cache_len,
    accepted_path,
    residual,
    norm_gain,
    out_weight,
    routes,
    route_weights,
    w_gate,
    w_up,
    w_down,
):
    place = lax.axis_index("cuts")
    tok_rows = queries.shape[0]
    requests = tok_rows // TREE
    cache_rows = cache_keys.shape[0] // requests
    width = queries.shape[1]
    attended = lax.map(
        tree_attention,
        (
            queries.reshape(requests, TREE, width),
            new_keys.reshape(requests, TREE, width),
            new_values.reshape(requests, TREE, width),
            cache_keys.reshape(requests, cache_rows, width),
            cache_values.reshape(requests, cache_rows, width),
            parents,
            tree_len,
            cache_len,
        ),
    )
    attended = attended.reshape(tok_rows, width)
    head_group = lax.all_to_all(attended, "cuts", split_axis=1, concat_axis=0, tiled=True)
    gate_full = lax.all_gather(w_gate[0], "cuts", axis=0)
    up_full = lax.all_gather(w_up[0], "cuts", axis=0)
    cut_count = lax.axis_size("cuts")
    half = width // 2
    down_early = w_down[0][:, :half]
    down_parts = [down_early] + [
        lax.ppermute(down_early, "cuts", [(i, (i + shift) % cut_count) for i in range(cut_count)])
        for shift in range(1, cut_count)
    ]
    down_late = lax.all_gather(w_down[0][:, half:], "cuts", axis=0)
    projected = jnp.dot(head_group, out_weight, preferred_element_type=jnp.float32)
    partials = lax.all_to_all(
        projected.astype(jnp.bfloat16).reshape(lax.axis_size("cuts"), tok_rows, width),
        "cuts",
        split_axis=0,
        concat_axis=0,
        tiled=True,
    )
    stream = residual.astype(jnp.float32) + jnp.sum(partials.astype(jnp.float32), axis=0)
    normed = norm_rows(stream, norm_gain)

    experts_all = w_gate.shape[0] * lax.axis_size("expert")
    capacity = CAP
    start = place * tok_rows
    own_routes = lax.dynamic_slice_in_dim(routes, start, tok_rows, 0)
    own_gains = lax.dynamic_slice_in_dim(route_weights, start, tok_rows, 0)
    flat = own_routes.reshape(tok_rows * TOPK)
    onehot = (flat[:, None] == jnp.arange(experts_all, dtype=jnp.int32)[None, :]).astype(jnp.int32)
    ahead = jnp.cumsum(onehot, axis=0) - onehot
    slot_of = jnp.sum(ahead * onehot, axis=1)
    dest = flat * capacity + slot_of
    token_of = jnp.arange(tok_rows * TOPK, dtype=jnp.int32) // TOPK
    table = jnp.full((experts_all * capacity,), -1, jnp.int32).at[dest].set(token_of)
    filled = table >= 0
    outgoing = jnp.where(
        filled[:, None], normed[jnp.maximum(table, 0)], jnp.zeros((), jnp.bfloat16)
    )
    outgoing = outgoing.reshape(experts_all, capacity, width)
    arrived = lax.all_to_all(outgoing, "expert", split_axis=0, concat_axis=0, tiled=True)
    rows = arrived.reshape(-1, width)
    gate = jnp.einsum("rd,cdf->rcf", rows, gate_full, preferred_element_type=jnp.float32)
    upper = jnp.einsum("rd,cdf->rcf", rows, up_full, preferred_element_type=jnp.float32)
    hidden = (jax.nn.silu(gate) * upper).astype(jnp.bfloat16)
    shift_of = (place - jnp.arange(cut_count, dtype=jnp.int32)) % cut_count
    down_by_owner = jnp.take(jnp.stack(down_parts), shift_of, axis=0)
    product = jnp.einsum("rcf,cfd->rd", hidden, down_by_owner, preferred_element_type=jnp.float32)
    returned_early = lax.all_to_all(
        product.astype(jnp.bfloat16).reshape(experts_all, capacity, half),
        "expert",
        split_axis=0,
        concat_axis=0,
        tiled=True,
    )
    product_late = jnp.einsum("rcf,cfd->rd", hidden, down_late, preferred_element_type=jnp.float32)
    returned_late = lax.all_to_all(
        product_late.astype(jnp.bfloat16).reshape(experts_all, capacity, half),
        "expert",
        split_axis=0,
        concat_axis=0,
        tiled=True,
    )
    route_major = dest.reshape(tok_rows, TOPK).T.reshape(-1)
    gains_route_major = own_gains.T[:, :, None]
    moe_parts = []
    for returned in (returned_early, returned_late):
        picked = returned.reshape(-1, half)[route_major].reshape(TOPK, tok_rows, half)
        moe_parts.append(jnp.sum(gains_route_major * picked.astype(jnp.float32), axis=0))
    moe = jnp.concatenate(moe_parts, axis=1)
    layer_out = (stream + moe).astype(jnp.bfloat16)
    picks = (jnp.arange(requests, dtype=jnp.int32)[:, None] * TREE + accepted_path).reshape(-1)
    accepted_kv = jnp.concatenate([new_keys[picks], new_values[picks]], axis=1)
    return (layer_out, accepted_kv)


def solution(mesh):
    placed = (
        P(("expert", "cuts"), None),
        P(("expert", "cuts"), None),
        P(("expert", "cuts"), None),
        P(("expert", "cuts"), None),
        P(("expert", "cuts"), None),
        P(("expert", "cuts"), None),
        P(("expert", "cuts")),
        P(("expert", "cuts")),
        P(("expert", "cuts"), None),
        P(("expert", "cuts"), None),
        P(),
        P("cuts", None),
        P("expert", None),
        P("expert", None),
        P("expert", None, "cuts"),
        P("expert", None, "cuts"),
        P("expert", "cuts", None),
    )
    return jax.shard_map(
        on_device,
        mesh=mesh,
        in_specs=placed,
        out_specs=(P(("expert", "cuts"), None), P(("expert", "cuts"), None)),
        check_vma=False,
    )
```

```python
import math

import jax
import jax.numpy as jnp
from jax import lax
from jax.sharding import PartitionSpec as P

HEADS = 16
HEAD = 128
TOPK = 4
TREE = 64
CAP = 8
N_CHUNKS = 2


epsilon = 1e-06


def ancestors(parents):
    slot_ids = jnp.arange(TREE, dtype=jnp.int32)
    linked = (parents[:, None] == slot_ids[None, :]) | (slot_ids[:, None] == slot_ids[None, :])
    reach = linked.astype(jnp.float32)
    for doubling in range(TREE.bit_length()):
        reach = jnp.minimum(jnp.dot(reach, reach, precision=lax.Precision.HIGHEST), 1.0)
    return reach > 0.5


def tree_attention(request):
    queries, new_keys, new_values, cache_keys, cache_values, parents, tree_len, cache_len = request
    cache_rows = cache_keys.shape[0]
    query_heads = queries.reshape(TREE, HEADS, HEAD)
    cache_heads = cache_keys.reshape(cache_rows, HEADS, HEAD)
    fresh_heads = new_keys.reshape(TREE, HEADS, HEAD)
    score_scale = 1.0 / math.sqrt(HEAD)
    cache_scores = (
        jnp.einsum("qhd,khd->hqk", query_heads, cache_heads, preferred_element_type=jnp.float32)
        * score_scale
    )
    fresh_scores = (
        jnp.einsum("qhd,khd->hqk", query_heads, fresh_heads, preferred_element_type=jnp.float32)
        * score_scale
    )
    slot_ids = jnp.arange(TREE, dtype=jnp.int32)
    cache_seen = jnp.arange(cache_rows, dtype=jnp.int32) < cache_len
    fresh_seen = ancestors(parents) & (slot_ids[None, :] < tree_len)
    cache_scores = jnp.where(cache_seen[None, None, :], cache_scores, -jnp.inf)
    fresh_scores = jnp.where(fresh_seen[None, :, :], fresh_scores, -jnp.inf)
    highest = jnp.maximum(jnp.max(cache_scores, axis=2), jnp.max(fresh_scores, axis=2))[:, :, None]
    cache_exp = jnp.exp(cache_scores - highest)
    fresh_exp = jnp.exp(fresh_scores - highest)
    total = jnp.sum(cache_exp, axis=2, keepdims=True) + jnp.sum(fresh_exp, axis=2, keepdims=True)
    cache_weights = (cache_exp / total).astype(jnp.bfloat16)
    fresh_weights = (fresh_exp / total).astype(jnp.bfloat16)
    mixed = jnp.einsum(
        "hqk,khd->qhd",
        cache_weights,
        cache_values.reshape(cache_rows, HEADS, HEAD),
        preferred_element_type=jnp.float32,
    )
    mixed = mixed + jnp.einsum(
        "hqk,khd->qhd",
        fresh_weights,
        new_values.reshape(TREE, HEADS, HEAD),
        preferred_element_type=jnp.float32,
    )
    return mixed.reshape(TREE, HEADS * HEAD).astype(jnp.bfloat16)


def expert_rows(flat_in, gate_w, up_w, down_w):
    gate = jnp.dot(flat_in, gate_w, preferred_element_type=jnp.float32)
    upper = jnp.dot(flat_in, up_w, preferred_element_type=jnp.float32)
    hidden = (jax.nn.silu(gate) * upper).astype(jnp.bfloat16)
    return jnp.dot(hidden, down_w, preferred_element_type=jnp.float32)


def norm_rows(stream, norm_gain):
    power = jnp.mean(stream * stream, axis=1, keepdims=True)
    return (stream * lax.rsqrt(power + epsilon) * norm_gain).astype(jnp.bfloat16)


def on_device(
    queries,
    new_keys,
    new_values,
    cache_keys,
    cache_values,
    parents,
    tree_len,
    cache_len,
    accepted_path,
    residual,
    norm_gain,
    out_weight,
    routes,
    route_weights,
    w_gate,
    w_up,
    w_down,
):
    place = lax.axis_index("cuts")
    tok_rows = queries.shape[0]
    requests = tok_rows // TREE
    cache_rows = cache_keys.shape[0] // requests
    width = queries.shape[1]
    attended = lax.map(
        tree_attention,
        (
            queries.reshape(requests, TREE, width),
            new_keys.reshape(requests, TREE, width),
            new_values.reshape(requests, TREE, width),
            cache_keys.reshape(requests, cache_rows, width),
            cache_values.reshape(requests, cache_rows, width),
            parents,
            tree_len,
            cache_len,
        ),
    )
    attended = attended.reshape(tok_rows, width)
    head_group = lax.all_to_all(attended, "cuts", split_axis=1, concat_axis=0, tiled=True)
    gate_full = lax.all_gather(w_gate[0], "cuts", axis=0)
    up_full = lax.all_gather(w_up[0], "cuts", axis=0)
    cut_count = lax.axis_size("cuts")
    half = width // 2
    down_early = w_down[0][:, :half]
    down_parts = [down_early] + [
        lax.ppermute(down_early, "cuts", [(i, (i + shift) % cut_count) for i in range(cut_count)])
        for shift in range(1, cut_count)
    ]
    down_late = lax.all_gather(w_down[0][:, half:], "cuts", axis=0)
    projected = jnp.dot(head_group, out_weight, preferred_element_type=jnp.float32)
    partials = lax.all_to_all(
        projected.astype(jnp.bfloat16).reshape(lax.axis_size("cuts"), tok_rows, width),
        "cuts",
        split_axis=0,
        concat_axis=0,
        tiled=True,
    )
    stream = residual.astype(jnp.float32) + jnp.sum(partials.astype(jnp.float32), axis=0)
    normed = norm_rows(stream, norm_gain)

    experts_all = w_gate.shape[0] * lax.axis_size("expert")
    capacity = CAP
    start = place * tok_rows
    own_routes = lax.dynamic_slice_in_dim(routes, start, tok_rows, 0)
    own_gains = lax.dynamic_slice_in_dim(route_weights, start, tok_rows, 0)
    flat = own_routes.reshape(tok_rows * TOPK)
    onehot = (flat[:, None] == jnp.arange(experts_all, dtype=jnp.int32)[None, :]).astype(jnp.int32)
    ahead = jnp.cumsum(onehot, axis=0) - onehot
    slot_of = jnp.sum(ahead * onehot, axis=1)
    dest = flat * capacity + slot_of
    token_of = jnp.arange(tok_rows * TOPK, dtype=jnp.int32) // TOPK
    table = jnp.full((experts_all * capacity,), -1, jnp.int32).at[dest].set(token_of)
    filled = table >= 0
    outgoing = jnp.where(
        filled[:, None], normed[jnp.maximum(table, 0)], jnp.zeros((), jnp.bfloat16)
    )
    outgoing = outgoing.reshape(experts_all, capacity, width)
    arrived = lax.all_to_all(outgoing, "expert", split_axis=0, concat_axis=0, tiled=True)
    rows = arrived.reshape(-1, width)
    gate = jnp.einsum("rd,cdf->rcf", rows, gate_full, preferred_element_type=jnp.float32)
    upper = jnp.einsum("rd,cdf->rcf", rows, up_full, preferred_element_type=jnp.float32)
    hidden = (jax.nn.silu(gate) * upper).astype(jnp.bfloat16)
    shift_of = (place - jnp.arange(cut_count, dtype=jnp.int32)) % cut_count
    down_by_owner = jnp.take(jnp.stack(down_parts), shift_of, axis=0)
    product = jnp.einsum("rcf,cfd->rd", hidden, down_by_owner, preferred_element_type=jnp.float32)
    returned_early = lax.all_to_all(
        product.astype(jnp.bfloat16).reshape(experts_all, capacity, half),
        "expert",
        split_axis=0,
        concat_axis=0,
        tiled=True,
    )
    product_late = jnp.einsum("rcf,cfd->rd", hidden, down_late, preferred_element_type=jnp.float32)
    returned_late = lax.all_to_all(
        product_late.astype(jnp.bfloat16).reshape(experts_all, capacity, half),
        "expert",
        split_axis=0,
        concat_axis=0,
        tiled=True,
    )
    slot_ids = jnp.arange(experts_all * capacity, dtype=jnp.int32)
    mixing = jnp.sum(
        jnp.where(
            dest.reshape(tok_rows, TOPK)[:, :, None] == slot_ids[None, None, :],
            own_gains[:, :, None],
            0.0,
        ),
        axis=1,
    )
    moe_parts = []
    for returned in (returned_early, returned_late):
        moe_parts.append(
            jnp.dot(
                mixing,
                returned.reshape(-1, half).astype(jnp.float32),
                precision=lax.Precision.HIGHEST,
                preferred_element_type=jnp.float32,
            )
        )
    moe = jnp.concatenate(moe_parts, axis=1)
    layer_out = (stream + moe).astype(jnp.bfloat16)
    picks = (jnp.arange(requests, dtype=jnp.int32)[:, None] * TREE + accepted_path).reshape(-1)
    accepted_kv = jnp.concatenate([new_keys[picks], new_values[picks]], axis=1)
    return (layer_out, accepted_kv)


def solution(mesh):
    placed = (
        P(("expert", "cuts"), None),
        P(("expert", "cuts"), None),
        P(("expert", "cuts"), None),
        P(("expert", "cuts"), None),
        P(("expert", "cuts"), None),
        P(("expert", "cuts"), None),
        P(("expert", "cuts")),
        P(("expert", "cuts")),
        P(("expert", "cuts"), None),
        P(("expert", "cuts"), None),
        P(),
        P("cuts", None),
        P("expert", None),
        P("expert", None),
        P("expert", None, "cuts"),
        P("expert", None, "cuts"),
        P("expert", "cuts", None),
    )
    return jax.shard_map(
        on_device,
        mesh=mesh,
        in_specs=placed,
        out_specs=(P(("expert", "cuts"), None), P(("expert", "cuts"), None)),
        check_vma=False,
    )
```

```python
import math

import jax
import jax.numpy as jnp
from jax import lax
from jax.sharding import PartitionSpec as P

HEADS = 16
HEAD = 128
TOPK = 4
TREE = 64
CAP = 8
N_CHUNKS = 2


epsilon = 1e-06


def ancestors(parents):
    slot_ids = jnp.arange(TREE, dtype=jnp.int32)
    linked = (parents[:, None] == slot_ids[None, :]) | (slot_ids[:, None] == slot_ids[None, :])
    reach = linked.astype(jnp.float32)
    for doubling in range(TREE.bit_length()):
        reach = jnp.minimum(jnp.dot(reach, reach, precision=lax.Precision.HIGHEST), 1.0)
    return reach > 0.5


def tree_attention(request):
    queries, new_keys, new_values, cache_keys, cache_values, parents, tree_len, cache_len = request
    cache_rows = cache_keys.shape[0]
    query_heads = queries.reshape(TREE, HEADS, HEAD)
    cache_heads = cache_keys.reshape(cache_rows, HEADS, HEAD)
    fresh_heads = new_keys.reshape(TREE, HEADS, HEAD)
    score_scale = 1.0 / math.sqrt(HEAD)
    cache_scores = (
        jnp.einsum("qhd,khd->hqk", query_heads, cache_heads, preferred_element_type=jnp.float32)
        * score_scale
    )
    fresh_scores = (
        jnp.einsum("qhd,khd->hqk", query_heads, fresh_heads, preferred_element_type=jnp.float32)
        * score_scale
    )
    slot_ids = jnp.arange(TREE, dtype=jnp.int32)
    cache_seen = jnp.arange(cache_rows, dtype=jnp.int32) < cache_len
    fresh_seen = ancestors(parents) & (slot_ids[None, :] < tree_len)
    cache_scores = jnp.where(cache_seen[None, None, :], cache_scores, -jnp.inf)
    fresh_scores = jnp.where(fresh_seen[None, :, :], fresh_scores, -jnp.inf)
    highest = jnp.maximum(jnp.max(cache_scores, axis=2), jnp.max(fresh_scores, axis=2))[:, :, None]
    cache_exp = jnp.exp(cache_scores - highest)
    fresh_exp = jnp.exp(fresh_scores - highest)
    total = jnp.sum(cache_exp, axis=2, keepdims=True) + jnp.sum(fresh_exp, axis=2, keepdims=True)
    cache_weights = (cache_exp / total).astype(jnp.bfloat16)
    fresh_weights = (fresh_exp / total).astype(jnp.bfloat16)
    mixed = jnp.einsum(
        "hqk,khd->qhd",
        cache_weights,
        cache_values.reshape(cache_rows, HEADS, HEAD),
        preferred_element_type=jnp.float32,
    )
    mixed = mixed + jnp.einsum(
        "hqk,khd->qhd",
        fresh_weights,
        new_values.reshape(TREE, HEADS, HEAD),
        preferred_element_type=jnp.float32,
    )
    return mixed.reshape(TREE, HEADS * HEAD).astype(jnp.bfloat16)


def expert_rows(flat_in, gate_w, up_w, down_w):
    gate = jnp.dot(flat_in, gate_w, preferred_element_type=jnp.float32)
    upper = jnp.dot(flat_in, up_w, preferred_element_type=jnp.float32)
    hidden = (jax.nn.silu(gate) * upper).astype(jnp.bfloat16)
    return jnp.dot(hidden, down_w, preferred_element_type=jnp.float32)


def norm_rows(stream, norm_gain):
    power = jnp.mean(stream * stream, axis=1, keepdims=True)
    return (stream * lax.rsqrt(power + epsilon) * norm_gain).astype(jnp.bfloat16)


def on_device(
    queries,
    new_keys,
    new_values,
    cache_keys,
    cache_values,
    parents,
    tree_len,
    cache_len,
    accepted_path,
    residual,
    norm_gain,
    out_weight,
    routes,
    route_weights,
    w_gate,
    w_up,
    w_down,
):
    place = lax.axis_index("cuts")
    tok_rows = queries.shape[0]
    requests = tok_rows // TREE
    cache_rows = cache_keys.shape[0] // requests
    width = queries.shape[1]
    attended = lax.map(
        tree_attention,
        (
            queries.reshape(requests, TREE, width),
            new_keys.reshape(requests, TREE, width),
            new_values.reshape(requests, TREE, width),
            cache_keys.reshape(requests, cache_rows, width),
            cache_values.reshape(requests, cache_rows, width),
            parents,
            tree_len,
            cache_len,
        ),
    )
    attended = attended.reshape(tok_rows, width)
    head_group = lax.all_to_all(attended, "cuts", split_axis=1, concat_axis=0, tiled=True)
    gate_full = lax.all_gather(w_gate[0], "cuts", axis=1, tiled=True)
    up_full = lax.all_gather(w_up[0], "cuts", axis=1, tiled=True)
    cut_count = lax.axis_size("cuts")
    half = width // 2
    down_early = w_down[0][:, :half]
    down_parts = [down_early] + [
        lax.ppermute(down_early, "cuts", [(i, (i + shift) % cut_count) for i in range(cut_count)])
        for shift in range(1, cut_count)
    ]
    down_late = lax.all_gather(w_down[0][:, half:], "cuts", axis=0)
    projected = jnp.dot(head_group, out_weight, preferred_element_type=jnp.float32)
    partials = lax.all_to_all(
        projected.astype(jnp.bfloat16).reshape(lax.axis_size("cuts"), tok_rows, width),
        "cuts",
        split_axis=0,
        concat_axis=0,
        tiled=True,
    )
    stream = residual.astype(jnp.float32) + jnp.sum(partials.astype(jnp.float32), axis=0)
    normed = norm_rows(stream, norm_gain)

    experts_all = w_gate.shape[0] * lax.axis_size("expert")
    capacity = CAP
    start = place * tok_rows
    own_routes = lax.dynamic_slice_in_dim(routes, start, tok_rows, 0)
    own_gains = lax.dynamic_slice_in_dim(route_weights, start, tok_rows, 0)
    flat = own_routes.reshape(tok_rows * TOPK)
    onehot = (flat[:, None] == jnp.arange(experts_all, dtype=jnp.int32)[None, :]).astype(jnp.int32)
    ahead = jnp.cumsum(onehot, axis=0) - onehot
    slot_of = jnp.sum(ahead * onehot, axis=1)
    dest = flat * capacity + slot_of
    token_of = jnp.arange(tok_rows * TOPK, dtype=jnp.int32) // TOPK
    table = jnp.full((experts_all * capacity,), -1, jnp.int32).at[dest].set(token_of)
    filled = table >= 0
    outgoing = jnp.where(
        filled[:, None], normed[jnp.maximum(table, 0)], jnp.zeros((), jnp.bfloat16)
    )
    outgoing = outgoing.reshape(experts_all, capacity, width)
    arrived = lax.all_to_all(outgoing, "expert", split_axis=0, concat_axis=0, tiled=True)
    rows = arrived.reshape(-1, width)
    gate = jnp.dot(rows, gate_full, preferred_element_type=jnp.float32)
    upper = jnp.dot(rows, up_full, preferred_element_type=jnp.float32)
    hidden = (jax.nn.silu(gate) * upper).astype(jnp.bfloat16).reshape(rows.shape[0], cut_count, -1)
    shift_of = (place - jnp.arange(cut_count, dtype=jnp.int32)) % cut_count
    down_by_owner = jnp.take(jnp.stack(down_parts), shift_of, axis=0)
    product = jnp.einsum("rcf,cfd->rd", hidden, down_by_owner, preferred_element_type=jnp.float32)
    returned_early = lax.all_to_all(
        product.astype(jnp.bfloat16).reshape(experts_all, capacity, half),
        "expert",
        split_axis=0,
        concat_axis=0,
        tiled=True,
    )
    product_late = jnp.einsum("rcf,cfd->rd", hidden, down_late, preferred_element_type=jnp.float32)
    returned_late = lax.all_to_all(
        product_late.astype(jnp.bfloat16).reshape(experts_all, capacity, half),
        "expert",
        split_axis=0,
        concat_axis=0,
        tiled=True,
    )
    slot_ids = jnp.arange(experts_all * capacity, dtype=jnp.int32)
    mixing = jnp.sum(
        jnp.where(
            dest.reshape(tok_rows, TOPK)[:, :, None] == slot_ids[None, None, :],
            own_gains[:, :, None],
            0.0,
        ),
        axis=1,
    )
    moe_parts = []
    for returned in (returned_early, returned_late):
        moe_parts.append(
            jnp.dot(
                mixing,
                returned.reshape(-1, half).astype(jnp.float32),
                precision=lax.Precision.HIGHEST,
                preferred_element_type=jnp.float32,
            )
        )
    moe = jnp.concatenate(moe_parts, axis=1)
    layer_out = (stream + moe).astype(jnp.bfloat16)
    picks = (jnp.arange(requests, dtype=jnp.int32)[:, None] * TREE + accepted_path).reshape(-1)
    accepted_kv = jnp.concatenate([new_keys[picks], new_values[picks]], axis=1)
    return (layer_out, accepted_kv)


def solution(mesh):
    placed = (
        P(("expert", "cuts"), None),
        P(("expert", "cuts"), None),
        P(("expert", "cuts"), None),
        P(("expert", "cuts"), None),
        P(("expert", "cuts"), None),
        P(("expert", "cuts"), None),
        P(("expert", "cuts")),
        P(("expert", "cuts")),
        P(("expert", "cuts"), None),
        P(("expert", "cuts"), None),
        P(),
        P("cuts", None),
        P("expert", None),
        P("expert", None),
        P("expert", None, "cuts"),
        P("expert", None, "cuts"),
        P("expert", "cuts", None),
    )
    return jax.shard_map(
        on_device,
        mesh=mesh,
        in_specs=placed,
        out_specs=(P(("expert", "cuts"), None), P(("expert", "cuts"), None)),
        check_vma=False,
    )
```
